128 devices in a mesh: row: 32 (over y, z_lo, x), col: 4 (over z_hi, core).
Axes of the slice: x: 4, y: 4, z: 4 (z_hi: 2, z_lo: 2; z = z_hi * 2 + z_lo), core: 2. Of those that a mesh axis runs over, the one named last changes fastest.
Arguments:
- ratings: bfloat16 [4, 262144, 512], P(None, ('row', 'col'))
- tile_mask: int32 [4, 2048, 4], P(None, ('row', 'col')), may hold values from 0 to 1, as said below
- tile_counts: int32 [128], replicated, may hold values from 1 to 16, as said below
- users: float32 [131072, 128], P(('row', 'col')), may hold values from -2 to 2
- user_accum: float32 [131072, 128], P(('row', 'col')), may hold values from 0.05 to 0.5
- items: float32 [65536, 128], P(('row', 'col')), may hold values from -2 to 2
- item_accum: float32 [65536, 128], P(('row', 'col')), may hold values from 0.05 to 0.5
Outputs:
- users_out: float32 [131072, 128], P(('row', 'col'))
- user_accum_out: float32 [131072, 128], P(('row', 'col'))
- items_out: float32 [65536, 128], P(('row', 'col'))
- item_accum_out: float32 [65536, 128], P(('row', 'col'))
- losses: float32 [4], replicated
The draws below stay inside these ranges and needn't reach their ends.
Inputs may be any that keep to these rules, and one draw needn't show every extreme that they name: Each group of 4 positions has tile_counts summing to 32, and exactly one position of each group, not always the same, owns 2 * 8 tiles. `tile_mask`: in each stratum, the first slot's first item tile of every position is 1.
All inputs are finite; a program needn't handle non-finite values.
Results may differ from the reference program's by a relative error of at most 0.0025.
Values sent between devices are 32-bit elements; how exact they have to be, the bound alone decides.
No kernel may reach another device: no remote copies, remote signals or barrier semaphores. Data moves between devices by JAX's collectives and lax.ppermute only.
A program may use at most 64 MiB of HBM per device.

```python
import math
import jax
import jax.numpy as jnp
from jax import lax

R = 128
TILE = 128
UT = 8
IT = 4
STRATA = 4
STEPS = 3
CAP = 16
GROUP = 4
LOOP = 128
USERS = 131072
ITEMS = 65536
N_ROW = 32
N_COL = 4


def draw_ratings(key, part):
    keys = jax.random.split(jax.random.fold_in(key, 11), 3)
    row_total = LOOP * CAP * TILE
    shape = (STRATA, row_total, IT * TILE)
    rise = 1.0 + 2.0 * jnp.arange(row_total, dtype=jnp.float32) / float(row_total)
    row_factor = jax.random.uniform(keys[1], (row_total,), jnp.float32, 0.6, 1.4)
    col_factor = jax.random.uniform(keys[2], (STRATA, 1, IT * TILE), jnp.float32, 0.6, 1.4)
    base = jax.random.normal(keys[0], shape, jnp.float32)
    values = base * (rise * row_factor)[None, :, None] * col_factor
    return values.astype(jnp.bfloat16)


def draw_tile_mask(key, part):
    keys = jax.random.split(jax.random.fold_in(key, 23), 2)
    level = jax.random.randint(keys[0], (STRATA, LOOP, 1, 1), 15, 95)
    rolled = jax.random.randint(keys[1], (STRATA, LOOP, CAP, IT), 0, 100)
    first = (jnp.arange(CAP)[:, None] == 0) & (jnp.arange(IT)[None, :] == 0)
    live_tiles = jnp.where(first[None, None], 1, (rolled < level).astype(jnp.int32))
    return live_tiles.reshape(STRATA, LOOP * CAP, IT).astype(jnp.int32)


def draw_tile_counts(key, part):
    keys = jax.random.split(jax.random.fold_in(key, 37), 2)
    group_count = LOOP // GROUP
    heavy = jax.random.randint(keys[0], (group_count, 1), 0, GROUP)
    pieces = jax.random.randint(keys[1], (group_count, 2), 1, UT)
    third = 2 * UT - pieces[:, 0:1] - pieces[:, 1:2]
    others = jnp.concatenate([pieces, third], axis=1)
    ranks = jnp.arange(GROUP, dtype=jnp.int32)[None, :]
    other_rank = jnp.clip(ranks - (ranks > heavy).astype(jnp.int32), 0, 2)
    picked = jnp.take_along_axis(others, other_rank, axis=1)
    values = jnp.where(ranks == heavy, 2 * UT, picked)
    return values.reshape(LOOP).astype(jnp.int32)


def block_scale(stream_key, dims, shards, least, top_value):
    factor_of, own = 1.0, jax.random.fold_in(stream_key, 6)
    for axis_at, shards_of in shards:
        heights = jnp.exp(jax.random.uniform(jax.random.fold_in(own, axis_at), (shards_of,), jnp.float32, least / len(shards), top_value / len(shards)))
        factor_of = factor_of * jnp.repeat(heights, dims[axis_at] // shards_of).reshape([-1 if axis == axis_at else 1 for axis in range(len(dims))])
    return factor_of


def normal_values(own_key, extent, deviation, reach, cuts=(), kind=jnp.bfloat16):
    array = deviation * jax.random.normal(own_key, extent, jnp.float32)
    if cuts:
        array = array * block_scale(own_key, extent, cuts, -0.22, 0.18)
    return jnp.clip(array, -reach, reach).astype(kind)


def setup_inputs(seed: int = 0) -> dict:
    key_list = jax.random.split(jax.random.key(seed), 8)
    ratings = draw_ratings(jax.random.fold_in(key_list[7], 71), 0)
    tile_mask = draw_tile_mask(jax.random.fold_in(key_list[7], 71), 0)
    tile_counts = draw_tile_counts(jax.random.fold_in(key_list[7], 71), 0)
    users = normal_values(key_list[3], (USERS, R), 0.3, 2.0, ((0, 128),), jnp.float32)
    user_accum = jnp.clip(jnp.exp(math.log(0.5) - 2.3025851 * jax.random.uniform(key_list[4], (USERS, R), jnp.float32) ** block_scale(key_list[4], (USERS, R), ((0, 128),), -0.2, 0.2)), 0.05, 0.5)
    items = normal_values(key_list[5], (ITEMS, R), 0.3, 2.0, ((0, 128),), jnp.float32)
    item_accum = jnp.clip(jnp.exp(math.log(0.5) - 2.3025851 * jax.random.uniform(key_list[6], (ITEMS, R), jnp.float32) ** block_scale(key_list[6], (ITEMS, R), ((0, 128),), -0.2, 0.2)), 0.05, 0.5)
    return dict(ratings=ratings, tile_mask=tile_mask, tile_counts=tile_counts, users=users, user_accum=user_accum, items=items, item_accum=item_accum)


ridge_weight = 0.02
step_rate = 0.05

def update(user_fac, user_acc, item_fac, item_acc, rating_block, live_tiles):
    tile_size = user_fac.shape[0] // live_tiles.shape[0]
    user_half = user_fac.astype(jnp.bfloat16)
    item_half = item_fac.astype(jnp.bfloat16)
    predicted = lax.dot_general(user_half, item_half, (((1,), (1,)), ((), ())), preferred_element_type=jnp.float32)
    residue = predicted - rating_block.astype(jnp.float32)
    masked = (residue.reshape(live_tiles.shape[0], tile_size, live_tiles.shape[1], tile_size) * live_tiles[:, None, :, None]).reshape(residue.shape)
    sq_error = jnp.sum(masked * residue)
    err_half = masked.astype(jnp.bfloat16)
    grad_user = jnp.dot(err_half, item_half, preferred_element_type=jnp.float32) * float(item_fac.shape[0]) ** (-0.5) + ridge_weight * user_fac
    grad_item = lax.dot_general(err_half, user_half, (((0,), (0,)), ((), ())), preferred_element_type=jnp.float32) * float(UT * TILE) ** (-0.5) + ridge_weight * item_fac
    user_acc = user_acc + grad_user * grad_user
    item_acc = item_acc + grad_item * grad_item
    user_fac = user_fac - step_rate * grad_user * lax.rsqrt(user_acc)
    item_fac = item_fac - step_rate * grad_item * lax.rsqrt(item_acc)
    return (user_fac, user_acc, item_fac, item_acc, sq_error)

def apply_update(packed):
    return update(packed[0], packed[1], packed[2], packed[3], packed[4], packed[5])

def reference(ratings, tile_mask, tile_counts, users, user_accum, items, item_accum):
    loop_len = N_ROW * N_COL
    slot_count = 2 * UT
    group_tiles = N_COL * UT
    item_rows = IT * TILE
    count_grid = tile_counts.reshape(N_ROW, N_COL)
    starts = (jnp.cumsum(count_grid, axis=1) - count_grid).reshape(loop_len).astype(jnp.int32)
    offsets = jnp.arange(slot_count, dtype=jnp.int32)
    local = (starts[:, None] + offsets[None, :]) % group_tiles
    group_base = jnp.arange(loop_len, dtype=jnp.int32) // N_COL * group_tiles
    tile_index = (group_base[:, None] + local).astype(jnp.int32)
    valid = offsets[None, :] < tile_counts[:, None]
    user_tiles = users.reshape(-1, TILE, R)
    acc_tiles = user_accum.reshape(-1, TILE, R)
    user_fac = user_tiles[tile_index].reshape(loop_len, slot_count * TILE, R)
    user_acc = acc_tiles[tile_index].reshape(loop_len, slot_count * TILE, R)
    item_fac = items.reshape(loop_len, item_rows, R)
    item_acc = item_accum.reshape(loop_len, item_rows, R)
    live_all = tile_mask.reshape(STRATA, loop_len, slot_count, IT).astype(jnp.float32) * valid.astype(jnp.float32)[None, :, :, None]
    rating_all = ratings.reshape(STRATA, loop_len, slot_count * TILE, item_rows)
    loss_list = []
    for stratum in range(STRATA):
        for inner in range(STEPS):
            user_fac, user_acc, item_fac, item_acc, sq_error = lax.map(apply_update, (user_fac, user_acc, item_fac, item_acc, rating_all[stratum], live_all[stratum]))
            if inner == 0:
                loss_list.append(jnp.sum(sq_error) / (jnp.sum(live_all[stratum]) * float(TILE * TILE)))
        if stratum + 1 < STRATA:
            item_fac = jnp.roll(item_fac, 1, 0)
            item_acc = jnp.roll(item_acc, 1, 0)
    total_tiles = USERS // TILE
    target = jnp.where(valid, tile_index, total_tiles).reshape(-1).astype(jnp.int32)
    users_new = jnp.zeros((total_tiles, TILE, R), user_fac.dtype).at[target].set(user_fac.reshape(-1, TILE, R), mode='drop')
    accum_new = jnp.zeros((total_tiles, TILE, R), user_acc.dtype).at[target].set(user_acc.reshape(-1, TILE, R), mode='drop')
    return (users_new.reshape(-1, R), accum_new.reshape(-1, R), item_fac.reshape(-1, R), item_acc.reshape(-1, R), jnp.stack(loss_list))
```

```python
import jax
import jax.numpy as jnp
from jax import lax
from jax.sharding import PartitionSpec as P

TILE = 128
UT = 8
STEPS = 3


ridge_weight = 0.02
step_rate = 0.05


def passed_along(value, axis, steps):
    count = lax.axis_size(axis)
    pairs = [(source, (source + steps) % count) for source in range(count)]
    return lax.ppermute(value, axis, pairs)


def update(user_fac, user_acc, item_fac, item_acc, rating_block, live_tiles):
    tile_size = user_fac.shape[0] // live_tiles.shape[0]
    user_half = user_fac.astype(jnp.bfloat16)
    item_half = item_fac.astype(jnp.bfloat16)
    predicted = lax.dot_general(
        user_half, item_half, (((1,), (1,)), ((), ())), preferred_element_type=jnp.float32
    )
    residue = predicted - rating_block.astype(jnp.float32)
    masked = (
        residue.reshape(live_tiles.shape[0], tile_size, live_tiles.shape[1], tile_size)
        * live_tiles[:, None, :, None]
    ).reshape(residue.shape)
    sq_error = jnp.sum(masked * residue)
    err_half = masked.astype(jnp.bfloat16)
    grad_user = (
        jnp.dot(err_half, item_half, preferred_element_type=jnp.float32)
        * float(item_fac.shape[0]) ** (-0.5)
        + ridge_weight * user_fac
    )
    grad_item = (
        lax.dot_general(
            err_half, user_half, (((0,), (0,)), ((), ())), preferred_element_type=jnp.float32
        )
        * float(UT * TILE) ** (-0.5)
        + ridge_weight * item_fac
    )
    user_acc = user_acc + grad_user * grad_user
    item_acc = item_acc + grad_item * grad_item
    user_fac = user_fac - step_rate * grad_user * lax.rsqrt(user_acc)
    item_fac = item_fac - step_rate * grad_item * lax.rsqrt(item_acc)
    return (user_fac, user_acc, item_fac, item_acc, sq_error)


def on_device(ratings, tile_mask, tile_counts, users, user_accum, items, item_accum):
    strata_count = ratings.shape[0]
    slot_count = tile_mask.shape[1]
    tile_size = ratings.shape[1] // slot_count
    group_size = lax.axis_size("col")
    member = lax.axis_index("col")
    arrived_rows = users.shape[0]
    group_counts = lax.dynamic_slice_in_dim(
        tile_counts, lax.axis_index("row") * group_size, group_size
    )
    ranks = jnp.arange(group_size, dtype=jnp.int32)
    start_tile = jnp.sum(jnp.where(ranks < member, group_counts, 0))
    own_count = jnp.sum(jnp.where(ranks == member, group_counts, 0))
    valid = (jnp.arange(slot_count, dtype=jnp.int32) < own_count).astype(jnp.float32)
    whole_pair = lax.all_gather(jnp.stack([users, user_accum]), "col", axis=1, tiled=True)
    pad_rows = slot_count * tile_size
    ext_pair = jnp.concatenate([whole_pair, whole_pair[:, :pad_rows]], axis=1)
    user_pair = lax.dynamic_slice_in_dim(ext_pair, start_tile * tile_size, pad_rows, 1)
    user_fac = user_pair[0]
    user_acc = user_pair[1]
    held_pair = jnp.stack([items, item_accum])
    loss_list = []
    for stratum in range(strata_count):
        live_tiles = tile_mask[stratum].astype(jnp.float32) * valid[:, None]
        item_fac = held_pair[0]
        item_acc = held_pair[1]
        for inner in range(STEPS):
            user_fac, user_acc, item_fac, item_acc, sq_error = update(
                user_fac, user_acc, item_fac, item_acc, ratings[stratum], live_tiles
            )
            if inner == 0:
                observed = jnp.sum(live_tiles) * float(tile_size * tile_size)
                loss_list.append(jnp.stack([sq_error, observed]))
        held_pair = jnp.stack([item_fac, item_acc])
        if stratum + 1 < strata_count:
            held_pair = passed_along(held_pair, ("row", "col"), 1)
    loss_parts = lax.psum(jnp.stack(loss_list), ("row", "col"))
    losses = loss_parts[:, 0] / loss_parts[:, 1]
    row_valid = jnp.repeat(valid, tile_size)[None, :, None] > 0.5
    kept_pair = jnp.where(row_valid, jnp.stack([user_fac, user_acc]), 0.0)
    frame_rows = group_size * arrived_rows + pad_rows
    frame_pair = lax.dynamic_update_slice_in_dim(
        jnp.zeros((2, frame_rows, kept_pair.shape[2]), jnp.float32),
        kept_pair,
        start_tile * tile_size,
        1,
    )
    users_pair = lax.psum_scatter(
        frame_pair[:, : group_size * arrived_rows], "col", scatter_dimension=1, tiled=True
    )
    return (users_pair[0], users_pair[1], held_pair[0], held_pair[1], losses)


def solution(mesh):
    return jax.shard_map(
        on_device,
        mesh=mesh,
        in_specs=(
            P(None, ("row", "col"), None),
            P(None, ("row", "col"), None),
            P(),
            P(("row", "col"), None),
            P(("row", "col"), None),
            P(("row", "col"), None),
            P(("row", "col"), None),
        ),
        out_specs=(
            P(("row", "col"), None),
            P(("row", "col"), None),
            P(("row", "col"), None),
            P(("row", "col"), None),
            P(),
        ),
        check_vma=False,
    )
```

```python
import jax
import jax.numpy as jnp
from jax import lax
from jax.sharding import PartitionSpec as P

TILE = 128
UT = 8
STEPS = 3


ridge_weight = 0.02
step_rate = 0.05


def passed_along(value, axis, steps):
    count = lax.axis_size(axis)
    pairs = [(source, (source + steps) % count) for source in range(count)]
    return lax.ppermute(value, axis, pairs)


def butterfly_sum(value, axis):
    count = lax.axis_size(axis)
    if count & (count - 1):
        return lax.psum(value, axis)
    stride = 1
    while stride < count:
        pairs = [(source, source ^ stride) for source in range(count)]
        value = value + lax.ppermute(value, axis, pairs)
        stride *= 2
    return value


def update(user_fac, user_acc, item_fac, item_acc, rating_block, live_tiles):
    tile_size = user_fac.shape[0] // live_tiles.shape[0]
    user_half = user_fac.astype(jnp.bfloat16)
    item_half = item_fac.astype(jnp.bfloat16)
    predicted = lax.dot_general(
        user_half, item_half, (((1,), (1,)), ((), ())), preferred_element_type=jnp.float32
    )
    residue = predicted - rating_block.astype(jnp.float32)
    masked = (
        residue.reshape(live_tiles.shape[0], tile_size, live_tiles.shape[1], tile_size)
        * live_tiles[:, None, :, None]
    ).reshape(residue.shape)
    sq_error = jnp.sum(masked * residue)
    err_half = masked.astype(jnp.bfloat16)
    grad_user = (
        jnp.dot(err_half, item_half, preferred_element_type=jnp.float32)
        * float(item_fac.shape[0]) ** (-0.5)
        + ridge_weight * user_fac
    )
    grad_item = (
        lax.dot_general(
            err_half, user_half, (((0,), (0,)), ((), ())), preferred_element_type=jnp.float32
        )
        * float(UT * TILE) ** (-0.5)
        + ridge_weight * item_fac
    )
    user_acc = user_acc + grad_user * grad_user
    item_acc = item_acc + grad_item * grad_item
    user_fac = user_fac - step_rate * grad_user * lax.rsqrt(user_acc)
    item_fac = item_fac - step_rate * grad_item * lax.rsqrt(item_acc)
    return (user_fac, user_acc, item_fac, item_acc, sq_error)


def on_device(ratings, tile_mask, tile_counts, users, user_accum, items, item_accum):
    strata_count = ratings.shape[0]
    slot_count = tile_mask.shape[1]
    tile_size = ratings.shape[1] // slot_count
    group_size = lax.axis_size("col")
    member = lax.axis_index("col")
    arrived_rows = users.shape[0]
    group_counts = lax.dynamic_slice_in_dim(
        tile_counts, lax.axis_index("row") * group_size, group_size
    )
    ranks = jnp.arange(group_size, dtype=jnp.int32)
    start_tile = jnp.sum(jnp.where(ranks < member, group_counts, 0))
    own_count = jnp.sum(jnp.where(ranks == member, group_counts, 0))
    valid = (jnp.arange(slot_count, dtype=jnp.int32) < own_count).astype(jnp.float32)
    whole_pair = lax.all_gather(jnp.stack([users, user_accum]), "col", axis=1, tiled=True)
    pad_rows = slot_count * tile_size
    ext_pair = jnp.concatenate([whole_pair, whole_pair[:, :pad_rows]], axis=1)
    user_pair = lax.dynamic_slice_in_dim(ext_pair, start_tile * tile_size, pad_rows, 1)
    user_fac = user_pair[0]
    user_acc = user_pair[1]
    held_pair = jnp.stack([items, item_accum])
    loss_list = []
    for stratum in range(strata_count):
        live_tiles = tile_mask[stratum].astype(jnp.float32) * valid[:, None]
        item_fac = held_pair[0]
        item_acc = held_pair[1]
        for inner in range(STEPS):
            user_fac, user_acc, item_fac, item_acc, sq_error = update(
                user_fac, user_acc, item_fac, item_acc, ratings[stratum], live_tiles
            )
            if inner == 0:
                observed = jnp.sum(live_tiles) * float(tile_size * tile_size)
                loss_list.append(jnp.stack([sq_error, observed]))
        held_pair = jnp.stack([item_fac, item_acc])
        if stratum + 1 < strata_count:
            held_pair = passed_along(held_pair, ("row", "col"), 1)
    loss_parts = butterfly_sum(jnp.stack(loss_list), ("row", "col"))
    losses = loss_parts[:, 0] / loss_parts[:, 1]
    row_valid = jnp.repeat(valid, tile_size)[None, :, None] > 0.5
    kept_pair = jnp.where(row_valid, jnp.stack([user_fac, user_acc]), 0.0)
    frame_rows = group_size * arrived_rows + pad_rows
    frame_pair = lax.dynamic_update_slice_in_dim(
        jnp.zeros((2, frame_rows, kept_pair.shape[2]), jnp.float32),
        kept_pair,
        start_tile * tile_size,
        1,
    )
    users_pair = lax.psum_scatter(
        frame_pair[:, : group_size * arrived_rows], "col", scatter_dimension=1, tiled=True
    )
    return (users_pair[0], users_pair[1], held_pair[0], held_pair[1], losses)


def solution(mesh):
    return jax.shard_map(
        on_device,
        mesh=mesh,
        in_specs=(
            P(None, ("row", "col"), None),
            P(None, ("row", "col"), None),
            P(),
            P(("row", "col"), None),
            P(("row", "col"), None),
            P(("row", "col"), None),
            P(("row", "col"), None),
        ),
        out_specs=(
            P(("row", "col"), None),
            P(("row", "col"), None),
            P(("row", "col"), None),
            P(("row", "col"), None),
            P(),
        ),
        check_vma=False,
    )
```

```python
import jax
import jax.numpy as jnp
from jax import lax
from jax.sharding import PartitionSpec as P
from jax.experimental import pallas as pl
from jax.experimental.pallas import tpu as pltpu

TILE = 128
UT = 8
STEPS = 3


ridge_weight = 0.02
step_rate = 0.05


def passed_along(value, axis, steps):
    count = lax.axis_size(axis)
    pairs = [(source, (source + steps) % count) for source in range(count)]
    return lax.ppermute(value, axis, pairs)


def butterfly_sum(value, axis):
    count = lax.axis_size(axis)
    if count & (count - 1):
        return lax.psum(value, axis)
    stride = 1
    while stride < count:
        pairs = [(source, source ^ stride) for source in range(count)]
        value = value + lax.ppermute(value, axis, pairs)
        stride *= 2
    return value


def update(user_fac, user_acc, item_fac, item_acc, rating_block, live_tiles):
    tile_size = user_fac.shape[0] // live_tiles.shape[0]
    user_half = user_fac.astype(jnp.bfloat16)
    item_half = item_fac.astype(jnp.bfloat16)
    predicted = lax.dot_general(
        user_half, item_half, (((1,), (1,)), ((), ())), preferred_element_type=jnp.float32
    )
    residue = predicted - rating_block.astype(jnp.float32)
    masked = (
        residue.reshape(live_tiles.shape[0], tile_size, live_tiles.shape[1], tile_size)
        * live_tiles[:, None, :, None]
    ).reshape(residue.shape)
    sq_error = jnp.sum(masked * residue)
    err_half = masked.astype(jnp.bfloat16)
    grad_user = (
        jnp.dot(err_half, item_half, preferred_element_type=jnp.float32)
        * float(item_fac.shape[0]) ** (-0.5)
        + ridge_weight * user_fac
    )
    grad_item = (
        lax.dot_general(
            err_half, user_half, (((0,), (0,)), ((), ())), preferred_element_type=jnp.float32
        )
        * float(UT * TILE) ** (-0.5)
        + ridge_weight * item_fac
    )
    user_acc = user_acc + grad_user * grad_user
    item_acc = item_acc + grad_item * grad_item
    user_fac = user_fac - step_rate * grad_user * lax.rsqrt(user_acc)
    item_fac = item_fac - step_rate * grad_item * lax.rsqrt(item_acc)
    return (user_fac, user_acc, item_fac, item_acc, sq_error)


CHUNK = 128


def stratum_kernel(
    mask_ref, rating_ref, u_in, gu_in, v_in, gv_in, u_ref, gu_ref, v_ref, gv_ref, sq_ref, gv_acc
):
    row_count = u_ref.shape[0]
    item_count = v_ref.shape[0]
    user_scale = float(item_count) ** (-0.5)
    item_scale = float(UT * TILE) ** (-0.5)
    u_ref[...] = u_in[...]
    gu_ref[...] = gu_in[...]
    v_ref[...] = v_in[...]
    gv_ref[...] = gv_in[...]
    sq_ref[...] = jnp.zeros(sq_ref.shape, jnp.float32)
    for inner in range(STEPS):
        item_half = v_ref[...].astype(jnp.bfloat16)
        gv_acc[...] = jnp.zeros(gv_acc.shape, jnp.float32)

        def body(chunk, carry, inner=inner, item_half=item_half):
            rows = pl.ds(pl.multiple_of(chunk * CHUNK, CHUNK), CHUNK)
            user_fac = u_ref[rows, :]
            user_acc = gu_ref[rows, :]
            user_half = user_fac.astype(jnp.bfloat16)
            predicted = lax.dot_general(
                user_half, item_half, (((1,), (1,)), ((), ())), preferred_element_type=jnp.float32
            )
            residue = predicted - rating_ref[rows, :].astype(jnp.float32)
            masked = residue * mask_ref[pl.ds(chunk, 1), :]
            if inner == 0:
                sq_ref[...] += jnp.sum(masked * residue, axis=0, keepdims=True)
            err_half = masked.astype(jnp.bfloat16)
            grad_user = (
                jnp.dot(err_half, item_half, preferred_element_type=jnp.float32) * user_scale
                + ridge_weight * user_fac
            )
            gv_acc[...] += lax.dot_general(
                err_half, user_half, (((0,), (0,)), ((), ())), preferred_element_type=jnp.float32
            )
            user_acc = user_acc + grad_user * grad_user
            u_ref[rows, :] = user_fac - step_rate * grad_user * lax.rsqrt(user_acc)
            gu_ref[rows, :] = user_acc
            return carry

        lax.fori_loop(0, row_count // CHUNK, body, 0)
        item_fac = v_ref[...]
        grad_item = gv_acc[...] * item_scale + ridge_weight * item_fac
        item_acc = gv_ref[...] + grad_item * grad_item
        gv_ref[...] = item_acc
        v_ref[...] = item_fac - step_rate * grad_item * lax.rsqrt(item_acc)


def run_stratum(stratum, ratings, mask_rows, user_fac, user_acc, item_fac, item_acc):
    rows, rank = user_fac.shape
    items_here = item_fac.shape[0]
    whole = lambda shape: pl.BlockSpec(shape, lambda i: (0,) * len(shape))
    outs = pl.pallas_call(
        stratum_kernel,
        grid=(1,),
        in_specs=[
            whole(mask_rows.shape),
            pl.BlockSpec((None, rows, items_here), lambda i: (stratum, 0, 0)),
            whole((rows, rank)),
            whole((rows, rank)),
            whole((items_here, rank)),
            whole((items_here, rank)),
        ],
        out_specs=[
            whole((rows, rank)),
            whole((rows, rank)),
            whole((items_here, rank)),
            whole((items_here, rank)),
            whole((1, items_here)),
        ],
        out_shape=[
            jax.ShapeDtypeStruct((rows, rank), jnp.float32),
            jax.ShapeDtypeStruct((rows, rank), jnp.float32),
            jax.ShapeDtypeStruct((items_here, rank), jnp.float32),
            jax.ShapeDtypeStruct((items_here, rank), jnp.float32),
            jax.ShapeDtypeStruct((1, items_here), jnp.float32),
        ],
        scratch_shapes=[pltpu.VMEM((items_here, rank), jnp.float32)],
        input_output_aliases={2: 0, 3: 1, 4: 2, 5: 3},
    )(mask_rows, ratings, user_fac, user_acc, item_fac, item_acc)
    return outs[0], outs[1], outs[2], outs[3], jnp.sum(outs[4])


def on_device(ratings, tile_mask, tile_counts, users, user_accum, items, item_accum):
    strata_count = ratings.shape[0]
    slot_count = tile_mask.shape[1]
    tile_size = ratings.shape[1] // slot_count
    group_size = lax.axis_size("col")
    member = lax.axis_index("col")
    arrived_rows = users.shape[0]
    group_counts = lax.dynamic_slice_in_dim(
        tile_counts, lax.axis_index("row") * group_size, group_size
    )
    ranks = jnp.arange(group_size, dtype=jnp.int32)
    start_tile = jnp.sum(jnp.where(ranks < member, group_counts, 0))
    own_count = jnp.sum(jnp.where(ranks == member, group_counts, 0))
    valid = (jnp.arange(slot_count, dtype=jnp.int32) < own_count).astype(jnp.float32)
    whole_pair = lax.all_gather(jnp.stack([users, user_accum]), "col", axis=1, tiled=True)
    pad_rows = slot_count * tile_size
    ext_pair = jnp.concatenate([whole_pair, whole_pair[:, :pad_rows]], axis=1)
    user_pair = lax.dynamic_slice_in_dim(ext_pair, start_tile * tile_size, pad_rows, 1)
    user_fac = user_pair[0]
    user_acc = user_pair[1]
    loss_list = []
    item_fac = items
    item_acc = item_accum
    for stratum in range(strata_count):
        live_tiles = tile_mask[stratum].astype(jnp.float32) * valid[:, None]
        mask_rows = jnp.repeat(live_tiles, tile_size, axis=1)
        user_fac, user_acc, item_fac, item_acc, sq_error = run_stratum(
            stratum, ratings, mask_rows, user_fac, user_acc, item_fac, item_acc
        )
        observed = jnp.sum(live_tiles) * float(tile_size * tile_size)
        loss_list.append(jnp.stack([sq_error, observed]))
        if stratum + 1 < strata_count:
            held_pair = passed_along(jnp.stack([item_fac, item_acc]), ("row", "col"), 1)
            item_fac = held_pair[0]
            item_acc = held_pair[1]
    loss_parts = butterfly_sum(jnp.stack(loss_list), ("row", "col"))
    losses = loss_parts[:, 0] / loss_parts[:, 1]
    row_valid = jnp.repeat(valid, tile_size)[None, :, None] > 0.5
    kept_pair = jnp.where(row_valid, jnp.stack([user_fac, user_acc]), 0.0)
    frame_rows = group_size * arrived_rows + pad_rows
    frame_pair = lax.dynamic_update_slice_in_dim(
        jnp.zeros((2, frame_rows, kept_pair.shape[2]), jnp.float32),
        kept_pair,
        start_tile * tile_size,
        1,
    )
    users_pair = lax.psum_scatter(
        frame_pair[:, : group_size * arrived_rows], "col", scatter_dimension=1, tiled=True
    )
    return (users_pair[0], users_pair[1], item_fac, item_acc, losses)


def solution(mesh):
    return jax.shard_map(
        on_device,
        mesh=mesh,
        in_specs=(
            P(None, ("row", "col"), None),
            P(None, ("row", "col"), None),
            P(),
            P(("row", "col"), None),
            P(("row", "col"), None),
            P(("row", "col"), None),
            P(("row", "col"), None),
        ),
        out_specs=(
            P(("row", "col"), None),
            P(("row", "col"), None),
            P(("row", "col"), None),
            P(("row", "col"), None),
            P(),
        ),
        check_vma=False,
    )
```

```python
from functools import partial

import jax
import jax.numpy as jnp
from jax import lax
from jax.sharding import PartitionSpec as P

TILE = 128
UT = 8
STEPS = 3


ridge_weight = 0.02
step_rate = 0.05


def passed_along(value, axis, steps):
    count = lax.axis_size(axis)
    pairs = [(source, (source + steps) % count) for source in range(count)]
    return lax.ppermute(value, axis, pairs)


def z_shift_pairs(mesh):
    grid = mesh.devices
    place = {}
    for row in range(grid.shape[0]):
        for col in range(grid.shape[1]):
            device = grid[row, col]
            place[(*device.coords, device.core_on_chip)] = row * grid.shape[1] + col
    depth = 1 + max(key[2] for key in place)
    pairs = []
    for (x, y, z, core), index in sorted(place.items(), key=lambda item: item[1]):
        step = 1 if core == 0 else -1
        pairs.append((index, place[(x, y, (z + step) % depth, core)]))
    return pairs


def core_swap(value):
    count = lax.axis_size("col")
    return lax.ppermute(value, "col", [(source, source ^ 1) for source in range(count)])


def far_chip(value, pairs):
    value = lax.ppermute(value, ("row", "col"), pairs)
    return lax.ppermute(value, ("row", "col"), pairs)


def butterfly_sum(value, axis):
    count = lax.axis_size(axis)
    if count & (count - 1):
        return lax.psum(value, axis)
    stride = 1
    while stride < count:
        pairs = [(source, source ^ stride) for source in range(count)]
        value = value + lax.ppermute(value, axis, pairs)
        stride *= 2
    return value


def update(user_fac, user_acc, item_fac, item_acc, rating_block, live_tiles):
    tile_size = user_fac.shape[0] // live_tiles.shape[0]
    user_half = user_fac.astype(jnp.bfloat16)
    item_half = item_fac.astype(jnp.bfloat16)
    predicted = lax.dot_general(
        user_half, item_half, (((1,), (1,)), ((), ())), preferred_element_type=jnp.float32
    )
    residue = predicted - rating_block.astype(jnp.float32)
    masked = (
        residue.reshape(live_tiles.shape[0], tile_size, live_tiles.shape[1], tile_size)
        * live_tiles[:, None, :, None]
    ).reshape(residue.shape)
    sq_error = jnp.sum(masked * residue)
    err_half = masked.astype(jnp.bfloat16)
    grad_user = (
        jnp.dot(err_half, item_half, preferred_element_type=jnp.float32)
        * float(item_fac.shape[0]) ** (-0.5)
        + ridge_weight * user_fac
    )
    grad_item = (
        lax.dot_general(
            err_half, user_half, (((0,), (0,)), ((), ())), preferred_element_type=jnp.float32
        )
        * float(UT * TILE) ** (-0.5)
        + ridge_weight * item_fac
    )
    user_acc = user_acc + grad_user * grad_user
    item_acc = item_acc + grad_item * grad_item
    user_fac = user_fac - step_rate * grad_user * lax.rsqrt(user_acc)
    item_fac = item_fac - step_rate * grad_item * lax.rsqrt(item_acc)
    return (user_fac, user_acc, item_fac, item_acc, sq_error)


def on_device(ratings, tile_mask, tile_counts, users, user_accum, items, item_accum, pairs=None):
    strata_count = ratings.shape[0]
    slot_count = tile_mask.shape[1]
    tile_size = ratings.shape[1] // slot_count
    group_size = lax.axis_size("col")
    member = lax.axis_index("col")
    arrived_rows = users.shape[0]
    group_counts = lax.dynamic_slice_in_dim(
        tile_counts, lax.axis_index("row") * group_size, group_size
    )
    ranks = jnp.arange(group_size, dtype=jnp.int32)
    start_tile = jnp.sum(jnp.where(ranks < member, group_counts, 0))
    own_count = jnp.sum(jnp.where(ranks == member, group_counts, 0))
    valid = (jnp.arange(slot_count, dtype=jnp.int32) < own_count).astype(jnp.float32)
    own = jnp.stack([users, user_accum])
    if pairs is None:
        whole_pair = lax.all_gather(own, "col", axis=1, tiled=True)
    else:
        partner = core_swap(own)
        far = far_chip(own, pairs)
        far_partner = core_swap(far)
        by_offset = jnp.stack([own, partner, far, far_partner])
        order = jnp.arange(group_size, dtype=jnp.int32) ^ member
        whole_pair = jnp.take(by_offset, order, axis=0)
        whole_pair = jnp.moveaxis(whole_pair, 0, 1).reshape(2, group_size * arrived_rows, -1)
    pad_rows = slot_count * tile_size
    ext_pair = jnp.concatenate([whole_pair, whole_pair[:, :pad_rows]], axis=1)
    user_pair = lax.dynamic_slice_in_dim(ext_pair, start_tile * tile_size, pad_rows, 1)
    user_fac = user_pair[0]
    user_acc = user_pair[1]
    held_pair = jnp.stack([items, item_accum])
    loss_list = []
    for stratum in range(strata_count):
        live_tiles = tile_mask[stratum].astype(jnp.float32) * valid[:, None]
        item_fac = held_pair[0]
        item_acc = held_pair[1]
        for inner in range(STEPS):
            user_fac, user_acc, item_fac, item_acc, sq_error = update(
                user_fac, user_acc, item_fac, item_acc, ratings[stratum], live_tiles
            )
            if inner == 0:
                observed = jnp.sum(live_tiles) * float(tile_size * tile_size)
                loss_list.append(jnp.stack([sq_error, observed]))
        held_pair = jnp.stack([item_fac, item_acc])
        if stratum + 1 < strata_count:
            held_pair = passed_along(held_pair, ("row", "col"), 1)
    loss_parts = butterfly_sum(jnp.stack(loss_list), ("row", "col"))
    losses = loss_parts[:, 0] / loss_parts[:, 1]
    row_valid = jnp.repeat(valid, tile_size)[None, :, None] > 0.5
    kept_pair = jnp.where(row_valid, jnp.stack([user_fac, user_acc]), 0.0)
    frame_rows = group_size * arrived_rows + pad_rows
    frame_pair = lax.dynamic_update_slice_in_dim(
        jnp.zeros((2, frame_rows, kept_pair.shape[2]), jnp.float32),
        kept_pair,
        start_tile * tile_size,
        1,
    )
    if pairs is None:
        users_pair = lax.psum_scatter(
            frame_pair[:, : group_size * arrived_rows], "col", scatter_dimension=1, tiled=True
        )
    else:
        blocks = frame_pair[:, : group_size * arrived_rows].reshape(2, group_size, arrived_rows, -1)
        order = jnp.arange(group_size, dtype=jnp.int32) ^ member
        by_offset = jnp.take(blocks, order, axis=1)
        from_partner = core_swap(jnp.stack([by_offset[:, 1], by_offset[:, 3]]))
        cross = by_offset[:, 2] + from_partner[1]
        from_far = far_chip(cross, pairs)
        users_pair = by_offset[:, 0] + from_partner[0] + from_far
    return (users_pair[0], users_pair[1], held_pair[0], held_pair[1], losses)


def solution(mesh):
    pairs = None
    if mesh.devices.shape[1] == 4 and hasattr(mesh.devices.flat[0], "coords"):
        pairs = z_shift_pairs(mesh)
    return jax.shard_map(
        partial(on_device, pairs=pairs),
        mesh=mesh,
        in_specs=(
            P(None, ("row", "col"), None),
            P(None, ("row", "col"), None),
            P(),
            P(("row", "col"), None),
            P(("row", "col"), None),
            P(("row", "col"), None),
            P(("row", "col"), None),
        ),
        out_specs=(
            P(("row", "col"), None),
            P(("row", "col"), None),
            P(("row", "col"), None),
            P(("row", "col"), None),
            P(),
        ),
        check_vma=False,
    )
```

```python
from functools import partial

import jax
import jax.numpy as jnp
from jax import lax
from jax.sharding import PartitionSpec as P

TILE = 128
UT = 8
STEPS = 3


ridge_weight = 0.02
step_rate = 0.05


def passed_along(value, axis, steps):
    count = lax.axis_size(axis)
    pairs = [(source, (source + steps) % count) for source in range(count)]
    return lax.ppermute(value, axis, pairs)


def z_shift_pairs(mesh):
    grid = mesh.devices
    place = {}
    for row in range(grid.shape[0]):
        for col in range(grid.shape[1]):
            device = grid[row, col]
            place[(*device.coords, device.core_on_chip)] = row * grid.shape[1] + col
    depth = 1 + max(key[2] for key in place)
    pairs = []
    for (x, y, z, core), index in sorted(place.items(), key=lambda item: item[1]):
        step = 1 if core == 0 else -1
        pairs.append((index, place[(x, y, (z + step) % depth, core)]))
    return pairs


def core_swap(value):
    count = lax.axis_size("col")
    return lax.ppermute(value, "col", [(source, source ^ 1) for source in range(count)])


def far_chip(value, pairs):
    value = lax.ppermute(value, ("row", "col"), pairs)
    return lax.ppermute(value, ("row", "col"), pairs)


def butterfly_sum(value, axis):
    count = lax.axis_size(axis)
    if count & (count - 1):
        return lax.psum(value, axis)
    stride = 1
    while stride < count:
        pairs = [(source, source ^ stride) for source in range(count)]
        value = value + lax.ppermute(value, axis, pairs)
        stride *= 2
    return value


def update(user_fac, user_acc, item_fac, item_acc, rating_block, live_tiles):
    tile_size = user_fac.shape[0] // live_tiles.shape[0]
    user_half = user_fac.astype(jnp.bfloat16)
    item_half = item_fac.astype(jnp.bfloat16)
    predicted = lax.dot_general(
        user_half, item_half, (((1,), (1,)), ((), ())), preferred_element_type=jnp.float32
    )
    residue = predicted - rating_block.astype(jnp.float32)
    masked = (
        residue.reshape(live_tiles.shape[0], tile_size, live_tiles.shape[1], tile_size)
        * live_tiles[:, None, :, None]
    ).reshape(residue.shape)
    sq_error = jnp.sum(masked * residue)
    err_half = masked.astype(jnp.bfloat16)
    grad_user = (
        jnp.dot(err_half, item_half, preferred_element_type=jnp.float32)
        * float(item_fac.shape[0]) ** (-0.5)
        + ridge_weight * user_fac
    )
    grad_item = (
        lax.dot_general(
            err_half, user_half, (((0,), (0,)), ((), ())), preferred_element_type=jnp.float32
        )
        * float(UT * TILE) ** (-0.5)
        + ridge_weight * item_fac
    )
    user_acc = user_acc + grad_user * grad_user
    item_acc = item_acc + grad_item * grad_item
    user_fac = user_fac - step_rate * grad_user * lax.rsqrt(user_acc)
    item_fac = item_fac - step_rate * grad_item * lax.rsqrt(item_acc)
    return (user_fac, user_acc, item_fac, item_acc, sq_error)


def on_device(ratings, tile_mask, tile_counts, users, user_accum, items, item_accum, pairs=None):
    strata_count = ratings.shape[0]
    slot_count = tile_mask.shape[1]
    tile_size = ratings.shape[1] // slot_count
    group_size = lax.axis_size("col")
    member = lax.axis_index("col")
    arrived_rows = users.shape[0]
    group_counts = lax.dynamic_slice_in_dim(
        tile_counts, lax.axis_index("row") * group_size, group_size
    )
    ranks = jnp.arange(group_size, dtype=jnp.int32)
    start_tile = jnp.sum(jnp.where(ranks < member, group_counts, 0))
    own_count = jnp.sum(jnp.where(ranks == member, group_counts, 0))
    valid = (jnp.arange(slot_count, dtype=jnp.int32) < own_count).astype(jnp.float32)
    if pairs is None:
        whole_pair = lax.all_gather(jnp.stack([users, user_accum]), "col", axis=1, tiled=True)
    else:
        whole_fac = lax.all_gather(users, "col", axis=0, tiled=True)
        partner = core_swap(user_accum)
        far = far_chip(user_accum, pairs)
        far_partner = core_swap(far)
        by_offset = jnp.stack([user_accum, partner, far, far_partner])
        order = jnp.arange(group_size, dtype=jnp.int32) ^ member
        whole_acc = jnp.take(by_offset, order, axis=0).reshape(group_size * arrived_rows, -1)
        whole_pair = jnp.stack([whole_fac, whole_acc])
    pad_rows = slot_count * tile_size
    ext_pair = jnp.concatenate([whole_pair, whole_pair[:, :pad_rows]], axis=1)
    user_pair = lax.dynamic_slice_in_dim(ext_pair, start_tile * tile_size, pad_rows, 1)
    user_fac = user_pair[0]
    user_acc = user_pair[1]
    held_pair = jnp.stack([items, item_accum])
    loss_list = []
    for stratum in range(strata_count):
        live_tiles = tile_mask[stratum].astype(jnp.float32) * valid[:, None]
        item_fac = held_pair[0]
        item_acc = held_pair[1]
        for inner in range(STEPS):
            user_fac, user_acc, item_fac, item_acc, sq_error = update(
                user_fac, user_acc, item_fac, item_acc, ratings[stratum], live_tiles
            )
            if inner == 0:
                observed = jnp.sum(live_tiles) * float(tile_size * tile_size)
                loss_list.append(jnp.stack([sq_error, observed]))
        held_pair = jnp.stack([item_fac, item_acc])
        if stratum + 1 < strata_count:
            held_pair = passed_along(held_pair, ("row", "col"), 1)
    loss_parts = butterfly_sum(jnp.stack(loss_list), ("row", "col"))
    losses = loss_parts[:, 0] / loss_parts[:, 1]
    row_valid = jnp.repeat(valid, tile_size)[None, :, None] > 0.5
    kept_pair = jnp.where(row_valid, jnp.stack([user_fac, user_acc]), 0.0)
    frame_rows = group_size * arrived_rows + pad_rows
    frame_pair = lax.dynamic_update_slice_in_dim(
        jnp.zeros((2, frame_rows, kept_pair.shape[2]), jnp.float32),
        kept_pair,
        start_tile * tile_size,
        1,
    )
    if pairs is None:
        users_pair = lax.psum_scatter(
            frame_pair[:, : group_size * arrived_rows], "col", scatter_dimension=1, tiled=True
        )
    else:
        users_fac = lax.psum_scatter(
            frame_pair[0, : group_size * arrived_rows], "col", scatter_dimension=0, tiled=True
        )
        blocks = frame_pair[1, : group_size * arrived_rows].reshape(group_size, arrived_rows, -1)
        order = jnp.arange(group_size, dtype=jnp.int32) ^ member
        by_offset = jnp.take(blocks, order, axis=0)
        from_partner = core_swap(jnp.stack([by_offset[1], by_offset[3]]))
        cross = by_offset[2] + from_partner[1]
        from_far = far_chip(cross, pairs)
        users_acc = by_offset[0] + from_partner[0] + from_far
        users_pair = jnp.stack([users_fac, users_acc])
    return (users_pair[0], users_pair[1], held_pair[0], held_pair[1], losses)


def solution(mesh):
    pairs = None
    if mesh.devices.shape[1] == 4 and hasattr(mesh.devices.flat[0], "coords"):
        pairs = z_shift_pairs(mesh)
    return jax.shard_map(
        partial(on_device, pairs=pairs),
        mesh=mesh,
        in_specs=(
            P(None, ("row", "col"), None),
            P(None, ("row", "col"), None),
            P(),
            P(("row", "col"), None),
            P(("row", "col"), None),
            P(("row", "col"), None),
            P(("row", "col"), None),
        ),
        out_specs=(
            P(("row", "col"), None),
            P(("row", "col"), None),
            P(("row", "col"), None),
            P(("row", "col"), None),
            P(),
        ),
        check_vma=False,
    )
```

```python
from functools import partial

import jax
import jax.numpy as jnp
from jax import lax
from jax.sharding import PartitionSpec as P

TILE = 128
UT = 8
STEPS = 3


ridge_weight = 0.02
step_rate = 0.05


def passed_along(value, axis, steps):
    count = lax.axis_size(axis)
    pairs = [(source, (source + steps) % count) for source in range(count)]
    return lax.ppermute(value, axis, pairs)


def z_shift_pairs(mesh):
    grid = mesh.devices
    place = {}
    for row in range(grid.shape[0]):
        for col in range(grid.shape[1]):
            device = grid[row, col]
            place[(*device.coords, device.core_on_chip)] = row * grid.shape[1] + col
    depth = 1 + max(key[2] for key in place)
    pairs = []
    for (x, y, z, core), index in sorted(place.items(), key=lambda item: item[1]):
        step = 1 if core == 0 else -1
        pairs.append((index, place[(x, y, (z + step) % depth, core)]))
    return pairs


def core_swap(value):
    count = lax.axis_size("col")
    return lax.ppermute(value, "col", [(source, source ^ 1) for source in range(count)])


def far_chip(value, pairs):
    value = lax.ppermute(value, ("row", "col"), pairs)
    return lax.ppermute(value, ("row", "col"), pairs)


def butterfly_sum(value, axis):
    count = lax.axis_size(axis)
    if count & (count - 1):
        return lax.psum(value, axis)
    stride = 1
    while stride < count:
        pairs = [(source, source ^ stride) for source in range(count)]
        value = value + lax.ppermute(value, axis, pairs)
        stride *= 2
    return value


def update(user_fac, user_acc, item_fac, item_acc, rating_block, live_tiles):
    tile_size = user_fac.shape[0] // live_tiles.shape[0]
    user_half = user_fac.astype(jnp.bfloat16)
    item_half = item_fac.astype(jnp.bfloat16)
    predicted = lax.dot_general(
        user_half, item_half, (((1,), (1,)), ((), ())), preferred_element_type=jnp.float32
    )
    residue = predicted - rating_block.astype(jnp.float32)
    masked = (
        residue.reshape(live_tiles.shape[0], tile_size, live_tiles.shape[1], tile_size)
        * live_tiles[:, None, :, None]
    ).reshape(residue.shape)
    sq_error = jnp.sum(masked * residue)
    err_half = masked.astype(jnp.bfloat16)
    grad_user = (
        jnp.dot(err_half, item_half, preferred_element_type=jnp.float32)
        * float(item_fac.shape[0]) ** (-0.5)
        + ridge_weight * user_fac
    )
    grad_item = (
        lax.dot_general(
            err_half, user_half, (((0,), (0,)), ((), ())), preferred_element_type=jnp.float32
        )
        * float(UT * TILE) ** (-0.5)
        + ridge_weight * item_fac
    )
    user_acc = user_acc + grad_user * grad_user
    item_acc = item_acc + grad_item * grad_item
    user_fac = user_fac - step_rate * grad_user * lax.rsqrt(user_acc)
    item_fac = item_fac - step_rate * grad_item * lax.rsqrt(item_acc)
    return (user_fac, user_acc, item_fac, item_acc, sq_error)


def on_device(ratings, tile_mask, tile_counts, users, user_accum, items, item_accum, pairs=None):
    strata_count = ratings.shape[0]
    slot_count = tile_mask.shape[1]
    tile_size = ratings.shape[1] // slot_count
    group_size = lax.axis_size("col")
    member = lax.axis_index("col")
    arrived_rows = users.shape[0]
    group_counts = lax.dynamic_slice_in_dim(
        tile_counts, lax.axis_index("row") * group_size, group_size
    )
    ranks = jnp.arange(group_size, dtype=jnp.int32)
    start_tile = jnp.sum(jnp.where(ranks < member, group_counts, 0))
    own_count = jnp.sum(jnp.where(ranks == member, group_counts, 0))
    valid = (jnp.arange(slot_count, dtype=jnp.int32) < own_count).astype(jnp.float32)
    if pairs is None:
        whole_pair = lax.all_gather(jnp.stack([users, user_accum]), "col", axis=1, tiled=True)
    else:
        whole_fac = lax.all_gather(users, "col", axis=0, tiled=True)
        partner = core_swap(user_accum)
        far = far_chip(user_accum, pairs)
        far_partner = core_swap(far)
        by_offset = jnp.stack([user_accum, partner, far, far_partner])
        order = jnp.arange(group_size, dtype=jnp.int32) ^ member
        whole_acc = jnp.take(by_offset, order, axis=0).reshape(group_size * arrived_rows, -1)
        whole_pair = jnp.stack([whole_fac, whole_acc])
    pad_rows = slot_count * tile_size
    ext_pair = jnp.concatenate([whole_pair, whole_pair[:, :pad_rows]], axis=1)
    user_pair = lax.dynamic_slice_in_dim(ext_pair, start_tile * tile_size, pad_rows, 1)
    user_fac = user_pair[0]
    user_acc = user_pair[1]
    item_fac = items
    item_acc = item_accum
    loss_list = []
    for stratum in range(strata_count):
        live_tiles = tile_mask[stratum].astype(jnp.float32) * valid[:, None]
        for inner in range(STEPS):
            user_fac, user_acc, item_fac, item_acc, sq_error = update(
                user_fac, user_acc, item_fac, item_acc, ratings[stratum], live_tiles
            )
            if inner == 0:
                observed = jnp.sum(live_tiles) * float(tile_size * tile_size)
                loss_list.append(jnp.stack([sq_error, observed]))
        if stratum + 1 < strata_count:
            item_fac, item_acc = passed_along((item_fac, item_acc), ("row", "col"), 1)
    loss_parts = butterfly_sum(jnp.stack(loss_list), ("row", "col"))
    losses = loss_parts[:, 0] / loss_parts[:, 1]
    row_valid = jnp.repeat(valid, tile_size)[None, :, None] > 0.5
    kept_pair = jnp.where(row_valid, jnp.stack([user_fac, user_acc]), 0.0)
    frame_rows = group_size * arrived_rows + pad_rows
    frame_pair = lax.dynamic_update_slice_in_dim(
        jnp.zeros((2, frame_rows, kept_pair.shape[2]), jnp.float32),
        kept_pair,
        start_tile * tile_size,
        1,
    )
    users_pair = lax.psum_scatter(
        frame_pair[:, : group_size * arrived_rows], "col", scatter_dimension=1, tiled=True
    )
    return (users_pair[0], users_pair[1], item_fac, item_acc, losses)


def solution(mesh):
    pairs = None
    if mesh.devices.shape[1] == 4 and hasattr(mesh.devices.flat[0], "coords"):
        pairs = z_shift_pairs(mesh)
    return jax.shard_map(
        partial(on_device, pairs=pairs),
        mesh=mesh,
        in_specs=(
            P(None, ("row", "col"), None),
            P(None, ("row", "col"), None),
            P(),
            P(("row", "col"), None),
            P(("row", "col"), None),
            P(("row", "col"), None),
            P(("row", "col"), None),
        ),
        out_specs=(
            P(("row", "col"), None),
            P(("row", "col"), None),
            P(("row", "col"), None),
            P(("row", "col"), None),
            P(),
        ),
        check_vma=False,
    )
```

```python
from functools import partial

import jax
import jax.numpy as jnp
from jax import lax
from jax.sharding import PartitionSpec as P

TILE = 128
UT = 8
STEPS = 3


ridge_weight = 0.02
step_rate = 0.05


def passed_along(value, axis, steps):
    count = lax.axis_size(axis)
    pairs = [(source, (source + steps) % count) for source in range(count)]
    return lax.ppermute(value, axis, pairs)


def z_shift_pairs(mesh):
    grid = mesh.devices
    place = {}
    for row in range(grid.shape[0]):
        for col in range(grid.shape[1]):
            device = grid[row, col]
            place[(*device.coords, device.core_on_chip)] = row * grid.shape[1] + col
    depth = 1 + max(key[2] for key in place)
    pairs = []
    for (x, y, z, core), index in sorted(place.items(), key=lambda item: item[1]):
        step = 1 if core == 0 else -1
        pairs.append((index, place[(x, y, (z + step) % depth, core)]))
    return pairs


def core_swap(value):
    count = lax.axis_size("col")
    return lax.ppermute(value, "col", [(source, source ^ 1) for source in range(count)])


def far_chip(value, pairs):
    value = lax.ppermute(value, ("row", "col"), pairs)
    return lax.ppermute(value, ("row", "col"), pairs)


def butterfly_sum(value, axis):
    count = lax.axis_size(axis)
    if count & (count - 1):
        return lax.psum(value, axis)
    stride = 1
    while stride < count:
        pairs = [(source, source ^ stride) for source in range(count)]
        value = value + lax.ppermute(value, axis, pairs)
        stride *= 2
    return value


def update(user_fac, user_acc, item_fac, item_acc, rating_block, live_tiles):
    tile_size = user_fac.shape[0] // live_tiles.shape[0]
    user_half = user_fac.astype(jnp.bfloat16)
    item_half = item_fac.astype(jnp.bfloat16)
    predicted = lax.dot_general(
        user_half, item_half, (((1,), (1,)), ((), ())), preferred_element_type=jnp.float32
    )
    residue = predicted - rating_block.astype(jnp.float32)
    masked = (
        residue.reshape(live_tiles.shape[0], tile_size, live_tiles.shape[1], tile_size)
        * live_tiles[:, None, :, None]
    ).reshape(residue.shape)
    sq_error = jnp.sum(masked * residue)
    err_half = masked.astype(jnp.bfloat16)
    grad_user = (
        jnp.dot(err_half, item_half, preferred_element_type=jnp.float32)
        * float(item_fac.shape[0]) ** (-0.5)
        + ridge_weight * user_fac
    )
    grad_item = (
        lax.dot_general(
            err_half, user_half, (((0,), (0,)), ((), ())), preferred_element_type=jnp.float32
        )
        * float(UT * TILE) ** (-0.5)
        + ridge_weight * item_fac
    )
    user_acc = user_acc + grad_user * grad_user
    item_acc = item_acc + grad_item * grad_item
    user_fac = user_fac - step_rate * grad_user * lax.rsqrt(user_acc)
    item_fac = item_fac - step_rate * grad_item * lax.rsqrt(item_acc)
    return (user_fac, user_acc, item_fac, item_acc, sq_error)


def on_device(ratings, tile_mask, tile_counts, users, user_accum, items, item_accum, pairs=None):
    strata_count = ratings.shape[0]
    slot_count = tile_mask.shape[1]
    tile_size = ratings.shape[1] // slot_count
    group_size = lax.axis_size("col")
    member = lax.axis_index("col")
    arrived_rows = users.shape[0]
    group_counts = lax.dynamic_slice_in_dim(
        tile_counts, lax.axis_index("row") * group_size, group_size
    )
    ranks = jnp.arange(group_size, dtype=jnp.int32)
    start_tile = jnp.sum(jnp.where(ranks < member, group_counts, 0))
    own_count = jnp.sum(jnp.where(ranks == member, group_counts, 0))
    valid = (jnp.arange(slot_count, dtype=jnp.int32) < own_count).astype(jnp.float32)
    tiles_each = arrived_rows // tile_size
    group_tiles = group_size * tiles_each
    rank = users.shape[1]
    group_tile = (start_tile + jnp.arange(slot_count, dtype=jnp.int32)) % group_tiles
    whole_fac = lax.all_gather(users, "col", axis=0, tiled=True)
    user_fac = whole_fac.reshape(group_tiles, tile_size, rank)[group_tile].reshape(-1, rank)
    if pairs is None:
        whole_acc = lax.all_gather(user_accum, "col", axis=0, tiled=True)
        user_acc = whole_acc.reshape(group_tiles, tile_size, rank)[group_tile].reshape(-1, rank)
    else:
        partner = core_swap(user_accum)
        far = far_chip(user_accum, pairs)
        far_partner = core_swap(far)
        by_offset = jnp.stack([user_accum, partner, far, far_partner]).reshape(
            group_size, tiles_each, tile_size, rank
        )
        offset = (group_tile // tiles_each) ^ member
        user_acc = by_offset[offset, group_tile % tiles_each].reshape(-1, rank)
    item_fac = items
    item_acc = item_accum
    loss_list = []
    for stratum in range(strata_count):
        live_tiles = tile_mask[stratum].astype(jnp.float32) * valid[:, None]
        for inner in range(STEPS):
            user_fac, user_acc, item_fac, item_acc, sq_error = update(
                user_fac, user_acc, item_fac, item_acc, ratings[stratum], live_tiles
            )
            if inner == 0:
                observed = jnp.sum(live_tiles) * float(tile_size * tile_size)
                loss_list.append(jnp.stack([sq_error, observed]))
        if stratum + 1 < strata_count:
            item_fac, item_acc = passed_along((item_fac, item_acc), ("row", "col"), 1)
    loss_parts = butterfly_sum(jnp.stack(loss_list), ("row", "col"))
    losses = loss_parts[:, 0] / loss_parts[:, 1]
    slot_of = jnp.arange(group_tiles, dtype=jnp.int32) - start_tile
    inside = (slot_of >= 0) & (slot_of < own_count)
    kept = jnp.stack([user_fac, user_acc]).reshape(2, slot_count, tile_size, rank)
    frame_pair = jnp.where(
        inside[None, :, None, None], kept[:, jnp.clip(slot_of, 0, slot_count - 1)], 0.0
    ).reshape(2, group_tiles * tile_size, rank)
    users_pair = lax.psum_scatter(frame_pair, "col", scatter_dimension=1, tiled=True)
    return (users_pair[0], users_pair[1], item_fac, item_acc, losses)


def solution(mesh):
    pairs = None
    if mesh.devices.shape[1] == 4 and hasattr(mesh.devices.flat[0], "coords"):
        pairs = z_shift_pairs(mesh)
    return jax.shard_map(
        partial(on_device, pairs=pairs),
        mesh=mesh,
        in_specs=(
            P(None, ("row", "col"), None),
            P(None, ("row", "col"), None),
            P(),
            P(("row", "col"), None),
            P(("row", "col"), None),
            P(("row", "col"), None),
            P(("row", "col"), None),
        ),
        out_specs=(
            P(("row", "col"), None),
            P(("row", "col"), None),
            P(("row", "col"), None),
            P(("row", "col"), None),
            P(),
        ),
        check_vma=False,
    )
```

```python
from functools import partial

import jax
import jax.numpy as jnp
from jax import lax
from jax.sharding import PartitionSpec as P

TILE = 128
UT = 8
STEPS = 3


ridge_weight = 0.02
step_rate = 0.05


def passed_along(value, axis, steps):
    count = lax.axis_size(axis)
    pairs = [(source, (source + steps) % count) for source in range(count)]
    return lax.ppermute(value, axis, pairs)


def z_shift_pairs(mesh):
    grid = mesh.devices
    place = {}
    for row in range(grid.shape[0]):
        for col in range(grid.shape[1]):
            device = grid[row, col]
            place[(*device.coords, device.core_on_chip)] = row * grid.shape[1] + col
    depth = 1 + max(key[2] for key in place)
    pairs = []
    for (x, y, z, core), index in sorted(place.items(), key=lambda item: item[1]):
        step = 1 if core == 0 else -1
        pairs.append((index, place[(x, y, (z + step) % depth, core)]))
    return pairs


def core_swap(value):
    count = lax.axis_size("col")
    return lax.ppermute(value, "col", [(source, source ^ 1) for source in range(count)])


def far_chip(value, pairs):
    value = lax.ppermute(value, ("row", "col"), pairs)
    return lax.ppermute(value, ("row", "col"), pairs)


def butterfly_sum(value, axis):
    count = lax.axis_size(axis)
    if count & (count - 1):
        return lax.psum(value, axis)
    stride = 1
    while stride < count:
        pairs = [(source, source ^ stride) for source in range(count)]
        value = value + lax.ppermute(value, axis, pairs)
        stride *= 2
    return value


def update(user_fac, user_acc, item_fac, item_acc, rating_block, live_tiles):
    tile_size = user_fac.shape[0] // live_tiles.shape[0]
    user_half = user_fac.astype(jnp.bfloat16)
    item_half = item_fac.astype(jnp.bfloat16)
    predicted = lax.dot_general(
        user_half, item_half, (((1,), (1,)), ((), ())), preferred_element_type=jnp.float32
    )
    residue = predicted - rating_block.astype(jnp.float32)
    masked = (
        residue.reshape(live_tiles.shape[0], tile_size, live_tiles.shape[1], tile_size)
        * live_tiles[:, None, :, None]
    ).reshape(residue.shape)
    sq_error = jnp.sum(masked * residue)
    err_half = masked.astype(jnp.bfloat16)
    grad_user = (
        jnp.dot(err_half, item_half, preferred_element_type=jnp.float32)
        * float(item_fac.shape[0]) ** (-0.5)
        + ridge_weight * user_fac
    )
    grad_item = (
        lax.dot_general(
            err_half, user_half, (((0,), (0,)), ((), ())), preferred_element_type=jnp.float32
        )
        * float(UT * TILE) ** (-0.5)
        + ridge_weight * item_fac
    )
    user_acc = user_acc + grad_user * grad_user
    item_acc = item_acc + grad_item * grad_item
    user_fac = user_fac - step_rate * grad_user * lax.rsqrt(user_acc)
    item_fac = item_fac - step_rate * grad_item * lax.rsqrt(item_acc)
    return (user_fac, user_acc, item_fac, item_acc, sq_error)


def on_device(ratings, tile_mask, tile_counts, users, user_accum, items, item_accum, pairs=None):
    strata_count = ratings.shape[0]
    slot_count = tile_mask.shape[1]
    tile_size = ratings.shape[1] // slot_count
    group_size = lax.axis_size("col")
    member = lax.axis_index("col")
    arrived_rows = users.shape[0]
    group_counts = lax.dynamic_slice_in_dim(
        tile_counts, lax.axis_index("row") * group_size, group_size
    )
    ranks = jnp.arange(group_size, dtype=jnp.int32)
    start_tile = jnp.sum(jnp.where(ranks < member, group_counts, 0))
    own_count = jnp.sum(jnp.where(ranks == member, group_counts, 0))
    valid = (jnp.arange(slot_count, dtype=jnp.int32) < own_count).astype(jnp.float32)
    tiles_each = arrived_rows // tile_size
    group_tiles = group_size * tiles_each
    rank = users.shape[1]
    group_tile = (start_tile + jnp.arange(slot_count, dtype=jnp.int32)) % group_tiles
    whole_fac = lax.all_gather(users, "col", axis=0, tiled=True)
    user_fac = whole_fac.reshape(group_tiles, tile_size, rank)[group_tile].reshape(-1, rank)
    if pairs is None:
        whole_acc = lax.all_gather(user_accum, "col", axis=0, tiled=True)
        user_acc = whole_acc.reshape(group_tiles, tile_size, rank)[group_tile].reshape(-1, rank)
    else:
        partner = core_swap(user_accum)
        far = far_chip(user_accum, pairs)
        far_partner = core_swap(far)
        by_offset = jnp.stack([user_accum, partner, far, far_partner]).reshape(
            group_size, tiles_each, tile_size, rank
        )
        offset = (group_tile // tiles_each) ^ member
        user_acc = by_offset[offset, group_tile % tiles_each].reshape(-1, rank)
    item_fac = items
    item_acc = item_accum
    loss_list = []
    for stratum in range(strata_count):
        live_tiles = tile_mask[stratum].astype(jnp.float32) * valid[:, None]
        for inner in range(STEPS):
            user_fac, user_acc, item_fac, item_acc, sq_error = update(
                user_fac, user_acc, item_fac, item_acc, ratings[stratum], live_tiles
            )
            if inner == 0:
                observed = jnp.sum(live_tiles) * float(tile_size * tile_size)
                loss_list.append(jnp.stack([sq_error, observed]))
        if stratum + 1 < strata_count:
            item_fac, item_acc = passed_along((item_fac, item_acc), ("row", "col"), 1)
    loss_parts = butterfly_sum(jnp.stack(loss_list), ("row", "col"))
    losses = loss_parts[:, 0] / loss_parts[:, 1]
    pad_rows = slot_count * tile_size
    row_valid = jnp.repeat(valid, tile_size)[None, :, None] > 0.5
    kept_pair = jnp.where(row_valid, jnp.stack([user_fac, user_acc]), 0.0)
    frame_rows = group_size * arrived_rows + pad_rows
    frame_pair = lax.dynamic_update_slice_in_dim(
        jnp.zeros((2, frame_rows, rank), jnp.float32), kept_pair, start_tile * tile_size, 1
    )
    users_pair = lax.psum_scatter(
        frame_pair[:, : group_size * arrived_rows], "col", scatter_dimension=1, tiled=True
    )
    return (users_pair[0], users_pair[1], item_fac, item_acc, losses)


def solution(mesh):
    pairs = None
    if mesh.devices.shape[1] == 4 and hasattr(mesh.devices.flat[0], "coords"):
        pairs = z_shift_pairs(mesh)
    return jax.shard_map(
        partial(on_device, pairs=pairs),
        mesh=mesh,
        in_specs=(
            P(None, ("row", "col"), None),
            P(None, ("row", "col"), None),
            P(),
            P(("row", "col"), None),
            P(("row", "col"), None),
            P(("row", "col"), None),
            P(("row", "col"), None),
        ),
        out_specs=(
            P(("row", "col"), None),
            P(("row", "col"), None),
            P(("row", "col"), None),
            P(("row", "col"), None),
            P(),
        ),
        check_vma=False,
    )
```

```python
from functools import partial

import jax
import jax.numpy as jnp
from jax import lax
from jax.sharding import PartitionSpec as P

TILE = 128
UT = 8
STEPS = 3


ridge_weight = 0.02
step_rate = 0.05


def passed_along(value, axis, steps):
    count = lax.axis_size(axis)
    pairs = [(source, (source + steps) % count) for source in range(count)]
    return lax.ppermute(value, axis, pairs)


def z_shift_pairs(mesh):
    grid = mesh.devices
    place = {}
    for row in range(grid.shape[0]):
        for col in range(grid.shape[1]):
            device = grid[row, col]
            place[(*device.coords, device.core_on_chip)] = row * grid.shape[1] + col
    depth = 1 + max(key[2] for key in place)
    pairs = []
    for (x, y, z, core), index in sorted(place.items(), key=lambda item: item[1]):
        step = 1 if core == 0 else -1
        pairs.append((index, place[(x, y, (z + step) % depth, core)]))
    return pairs


def core_swap(value):
    count = lax.axis_size("col")
    return lax.ppermute(value, "col", [(source, source ^ 1) for source in range(count)])


def far_chip(value, pairs):
    value = lax.ppermute(value, ("row", "col"), pairs)
    return lax.ppermute(value, ("row", "col"), pairs)


def butterfly_sum(value, axis):
    count = lax.axis_size(axis)
    if count & (count - 1):
        return lax.psum(value, axis)
    stride = 1
    while stride < count:
        pairs = [(source, source ^ stride) for source in range(count)]
        value = value + lax.ppermute(value, axis, pairs)
        stride *= 2
    return value


def update(user_fac, user_acc, item_fac, item_acc, rating_block, live_tiles):
    tile_size = user_fac.shape[0] // live_tiles.shape[0]
    user_half = user_fac.astype(jnp.bfloat16)
    item_half = item_fac.astype(jnp.bfloat16)
    predicted = lax.dot_general(
        user_half, item_half, (((1,), (1,)), ((), ())), preferred_element_type=jnp.float32
    )
    residue = predicted - rating_block.astype(jnp.float32)
    masked = (
        residue.reshape(live_tiles.shape[0], tile_size, live_tiles.shape[1], tile_size)
        * live_tiles[:, None, :, None]
    ).reshape(residue.shape)
    sq_error = jnp.sum(masked * residue)
    err_half = masked.astype(jnp.bfloat16)
    grad_user = (
        jnp.dot(err_half, item_half, preferred_element_type=jnp.float32)
        * float(item_fac.shape[0]) ** (-0.5)
        + ridge_weight * user_fac
    )
    grad_item = (
        lax.dot_general(
            err_half, user_half, (((0,), (0,)), ((), ())), preferred_element_type=jnp.float32
        )
        * float(UT * TILE) ** (-0.5)
        + ridge_weight * item_fac
    )
    user_acc = user_acc + grad_user * grad_user
    item_acc = item_acc + grad_item * grad_item
    user_fac = user_fac - step_rate * grad_user * lax.rsqrt(user_acc)
    item_fac = item_fac - step_rate * grad_item * lax.rsqrt(item_acc)
    return (user_fac, user_acc, item_fac, item_acc, sq_error)


def on_device(ratings, tile_mask, tile_counts, users, user_accum, items, item_accum, pairs=None):
    strata_count = ratings.shape[0]
    slot_count = tile_mask.shape[1]
    tile_size = ratings.shape[1] // slot_count
    group_size = lax.axis_size("col")
    member = lax.axis_index("col")
    arrived_rows = users.shape[0]
    group_counts = lax.dynamic_slice_in_dim(
        tile_counts, lax.axis_index("row") * group_size, group_size
    )
    ranks = jnp.arange(group_size, dtype=jnp.int32)
    start_tile = jnp.sum(jnp.where(ranks < member, group_counts, 0))
    own_count = jnp.sum(jnp.where(ranks == member, group_counts, 0))
    valid = (jnp.arange(slot_count, dtype=jnp.int32) < own_count).astype(jnp.float32)
    tiles_each = arrived_rows // tile_size
    group_tiles = group_size * tiles_each
    rank = users.shape[1]
    group_tile = (start_tile + jnp.arange(slot_count, dtype=jnp.int32)) % group_tiles
    whole_fac = lax.all_gather(users, "col", axis=0, tiled=True)
    user_fac = whole_fac.reshape(group_tiles, tile_size, rank)[group_tile].reshape(-1, rank)
    if pairs is None:
        whole_acc = lax.all_gather(user_accum, "col", axis=0, tiled=True)
        user_acc = whole_acc.reshape(group_tiles, tile_size, rank)[group_tile].reshape(-1, rank)
    else:
        partner = core_swap(user_accum)
        far = far_chip(user_accum, pairs)
        far_partner = core_swap(far)
        by_offset = jnp.stack([user_accum, partner, far, far_partner]).reshape(
            group_size, tiles_each, tile_size, rank
        )
        offset = (group_tile // tiles_each) ^ member
        user_acc = by_offset[offset, group_tile % tiles_each].reshape(-1, rank)
    item_fac = items
    item_acc = item_accum
    loss_list = []
    for stratum in range(strata_count):
        live_tiles = tile_mask[stratum].astype(jnp.float32) * valid[:, None]
        for inner in range(STEPS):
            user_fac, user_acc, item_fac, item_acc, sq_error = update(
                user_fac, user_acc, item_fac, item_acc, ratings[stratum], live_tiles
            )
            if inner == 0:
                observed = jnp.sum(live_tiles) * float(tile_size * tile_size)
                loss_list.append(jnp.stack([sq_error, observed]))
        if stratum + 1 < strata_count:
            half = item_fac.shape[0] // 2
            pieces = passed_along(
                (item_fac[:half], item_fac[half:], item_acc[:half], item_acc[half:]),
                ("row", "col"),
                1,
            )
            item_fac = jnp.concatenate(pieces[:2], axis=0)
            item_acc = jnp.concatenate(pieces[2:], axis=0)
    loss_parts = butterfly_sum(jnp.stack(loss_list), ("row", "col"))
    losses = loss_parts[:, 0] / loss_parts[:, 1]
    pad_rows = slot_count * tile_size
    row_valid = jnp.repeat(valid, tile_size)[None, :, None] > 0.5
    kept_pair = jnp.where(row_valid, jnp.stack([user_fac, user_acc]), 0.0)
    frame_rows = group_size * arrived_rows + pad_rows
    frame_pair = lax.dynamic_update_slice_in_dim(
        jnp.zeros((2, frame_rows, rank), jnp.float32), kept_pair, start_tile * tile_size, 1
    )
    users_pair = lax.psum_scatter(
        frame_pair[:, : group_size * arrived_rows], "col", scatter_dimension=1, tiled=True
    )
    return (users_pair[0], users_pair[1], item_fac, item_acc, losses)


def solution(mesh):
    pairs = None
    if mesh.devices.shape[1] == 4 and hasattr(mesh.devices.flat[0], "coords"):
        pairs = z_shift_pairs(mesh)
    return jax.shard_map(
        partial(on_device, pairs=pairs),
        mesh=mesh,
        in_specs=(
            P(None, ("row", "col"), None),
            P(None, ("row", "col"), None),
            P(),
            P(("row", "col"), None),
            P(("row", "col"), None),
            P(("row", "col"), None),
            P(("row", "col"), None),
        ),
        out_specs=(
            P(("row", "col"), None),
            P(("row", "col"), None),
            P(("row", "col"), None),
            P(("row", "col"), None),
            P(),
        ),
        check_vma=False,
    )
```

```python
from functools import partial

import jax
import jax.numpy as jnp
from jax import lax
from jax.sharding import PartitionSpec as P

TILE = 128
UT = 8
STEPS = 3


ridge_weight = 0.02
step_rate = 0.05


def passed_along(value, axis, steps):
    count = lax.axis_size(axis)
    pairs = [(source, (source + steps) % count) for source in range(count)]
    return lax.ppermute(value, axis, pairs)


def z_shift_pairs(mesh):
    grid = mesh.devices
    place = {}
    for row in range(grid.shape[0]):
        for col in range(grid.shape[1]):
            device = grid[row, col]
            place[(*device.coords, device.core_on_chip)] = row * grid.shape[1] + col
    depth = 1 + max(key[2] for key in place)
    pairs = []
    for (x, y, z, core), index in sorted(place.items(), key=lambda item: item[1]):
        step = 1 if core == 0 else -1
        pairs.append((index, place[(x, y, (z + step) % depth, core)]))
    return pairs


def core_swap(value):
    count = lax.axis_size("col")
    return lax.ppermute(value, "col", [(source, source ^ 1) for source in range(count)])


def far_chip(value, pairs):
    value = lax.ppermute(value, ("row", "col"), pairs)
    return lax.ppermute(value, ("row", "col"), pairs)


def butterfly_sum(value, axis):
    count = lax.axis_size(axis)
    if count & (count - 1):
        return lax.psum(value, axis)
    index = lax.axis_index(axis)
    stride = 1
    while stride < count:
        radix = 4 if count // stride >= 4 else 2
        digit = (index // stride) % radix
        received = [value]
        for shift in range(1, radix):
            pairs = []
            for source in range(count):
                source_digit = (source // stride) % radix
                target = source + (((source_digit + shift) % radix) - source_digit) * stride
                pairs.append((source, target))
            received.append(lax.ppermute(value, axis, pairs))
        received = jnp.stack(received)
        total = received[(digit - 0) % radix]
        for place in range(1, radix):
            total = total + received[(digit - place) % radix]
        value = total
        stride *= radix
    return value


def update(user_fac, user_acc, item_fac, item_acc, rating_block, live_tiles):
    tile_size = user_fac.shape[0] // live_tiles.shape[0]
    user_half = user_fac.astype(jnp.bfloat16)
    item_half = item_fac.astype(jnp.bfloat16)
    predicted = lax.dot_general(
        user_half, item_half, (((1,), (1,)), ((), ())), preferred_element_type=jnp.float32
    )
    residue = predicted - rating_block.astype(jnp.float32)
    masked = (
        residue.reshape(live_tiles.shape[0], tile_size, live_tiles.shape[1], tile_size)
        * live_tiles[:, None, :, None]
    ).reshape(residue.shape)
    sq_error = jnp.sum(masked * residue)
    err_half = masked.astype(jnp.bfloat16)
    grad_user = (
        jnp.dot(err_half, item_half, preferred_element_type=jnp.float32)
        * float(item_fac.shape[0]) ** (-0.5)
        + ridge_weight * user_fac
    )
    grad_item = (
        lax.dot_general(
            err_half, user_half, (((0,), (0,)), ((), ())), preferred_element_type=jnp.float32
        )
        * float(UT * TILE) ** (-0.5)
        + ridge_weight * item_fac
    )
    user_acc = user_acc + grad_user * grad_user
    item_acc = item_acc + grad_item * grad_item
    user_fac = user_fac - step_rate * grad_user * lax.rsqrt(user_acc)
    item_fac = item_fac - step_rate * grad_item * lax.rsqrt(item_acc)
    return (user_fac, user_acc, item_fac, item_acc, sq_error)


def on_device(ratings, tile_mask, tile_counts, users, user_accum, items, item_accum, pairs=None):
    strata_count = ratings.shape[0]
    slot_count = tile_mask.shape[1]
    tile_size = ratings.shape[1] // slot_count
    group_size = lax.axis_size("col")
    member = lax.axis_index("col")
    arrived_rows = users.shape[0]
    group_counts = lax.dynamic_slice_in_dim(
        tile_counts, lax.axis_index("row") * group_size, group_size
    )
    ranks = jnp.arange(group_size, dtype=jnp.int32)
    start_tile = jnp.sum(jnp.where(ranks < member, group_counts, 0))
    own_count = jnp.sum(jnp.where(ranks == member, group_counts, 0))
    valid = (jnp.arange(slot_count, dtype=jnp.int32) < own_count).astype(jnp.float32)
    tiles_each = arrived_rows // tile_size
    group_tiles = group_size * tiles_each
    rank = users.shape[1]
    group_tile = (start_tile + jnp.arange(slot_count, dtype=jnp.int32)) % group_tiles
    whole_fac = lax.all_gather(users, "col", axis=0, tiled=True)
    user_fac = whole_fac.reshape(group_tiles, tile_size, rank)[group_tile].reshape(-1, rank)
    if pairs is None:
        whole_acc = lax.all_gather(user_accum, "col", axis=0, tiled=True)
        user_acc = whole_acc.reshape(group_tiles, tile_size, rank)[group_tile].reshape(-1, rank)
    else:
        partner = core_swap(user_accum)
        far = far_chip(user_accum, pairs)
        far_partner = core_swap(far)
        by_offset = jnp.stack([user_accum, partner, far, far_partner]).reshape(
            group_size, tiles_each, tile_size, rank
        )
        offset = (group_tile // tiles_each) ^ member
        user_acc = by_offset[offset, group_tile % tiles_each].reshape(-1, rank)
    item_fac = items
    item_acc = item_accum
    loss_list = []
    for stratum in range(strata_count):
        live_tiles = tile_mask[stratum].astype(jnp.float32) * valid[:, None]
        for inner in range(STEPS):
            user_fac, user_acc, item_fac, item_acc, sq_error = update(
                user_fac, user_acc, item_fac, item_acc, ratings[stratum], live_tiles
            )
            if inner == 0:
                observed = jnp.sum(live_tiles) * float(tile_size * tile_size)
                loss_list.append(jnp.stack([sq_error, observed]))
        if stratum + 1 < strata_count:
            item_fac, item_acc = passed_along((item_fac, item_acc), ("row", "col"), 1)
    loss_parts = butterfly_sum(jnp.stack(loss_list), ("row", "col"))
    losses = loss_parts[:, 0] / loss_parts[:, 1]
    pad_rows = slot_count * tile_size
    row_valid = jnp.repeat(valid, tile_size)[None, :, None] > 0.5
    kept_pair = jnp.where(row_valid, jnp.stack([user_fac, user_acc]), 0.0)
    frame_rows = group_size * arrived_rows + pad_rows
    frame_pair = lax.dynamic_update_slice_in_dim(
        jnp.zeros((2, frame_rows, rank), jnp.float32), kept_pair, start_tile * tile_size, 1
    )
    if pairs is None:
        users_pair = lax.psum_scatter(
            frame_pair[:, : group_size * arrived_rows], "col", scatter_dimension=1, tiled=True
        )
        users_new, accum_new = users_pair[0], users_pair[1]
    else:
        users_new = lax.psum_scatter(
            frame_pair[0, : group_size * arrived_rows], "col", scatter_dimension=0, tiled=True
        )
        blocks = frame_pair[1, : group_size * arrived_rows].reshape(group_size, arrived_rows, rank)
        order = jnp.arange(group_size, dtype=jnp.int32) ^ member
        by_offset = jnp.take(blocks, order, axis=0)
        from_partner = core_swap(jnp.stack([by_offset[1], by_offset[3]]))
        cross = by_offset[2] + from_partner[1]
        from_far = far_chip(cross, pairs)
        accum_new = by_offset[0] + from_partner[0] + from_far
    return (users_new, accum_new, item_fac, item_acc, losses)


def solution(mesh):
    pairs = None
    if mesh.devices.shape[1] == 4 and hasattr(mesh.devices.flat[0], "coords"):
        pairs = z_shift_pairs(mesh)
    return jax.shard_map(
        partial(on_device, pairs=pairs),
        mesh=mesh,
        in_specs=(
            P(None, ("row", "col"), None),
            P(None, ("row", "col"), None),
            P(),
            P(("row", "col"), None),
            P(("row", "col"), None),
            P(("row", "col"), None),
            P(("row", "col"), None),
        ),
        out_specs=(
            P(("row", "col"), None),
            P(("row", "col"), None),
            P(("row", "col"), None),
            P(("row", "col"), None),
            P(),
        ),
        check_vma=False,
    )
```

```python
from functools import partial

import jax
import jax.numpy as jnp
from jax import lax
from jax.sharding import PartitionSpec as P

TILE = 128
UT = 8
STEPS = 3


ridge_weight = 0.02
step_rate = 0.05


def passed_along(value, axis, steps):
    count = lax.axis_size(axis)
    pairs = [(source, (source + steps) % count) for source in range(count)]
    return lax.ppermute(value, axis, pairs)


def z_shift_pairs(mesh):
    grid = mesh.devices
    place = {}
    for row in range(grid.shape[0]):
        for col in range(grid.shape[1]):
            device = grid[row, col]
            place[(*device.coords, device.core_on_chip)] = row * grid.shape[1] + col
    depth = 1 + max(key[2] for key in place)
    pairs = []
    for (x, y, z, core), index in sorted(place.items(), key=lambda item: item[1]):
        step = 1 if core == 0 else -1
        pairs.append((index, place[(x, y, (z + step) % depth, core)]))
    return pairs


def core_swap(value):
    count = lax.axis_size("col")
    return lax.ppermute(value, "col", [(source, source ^ 1) for source in range(count)])


def far_chip(value, pairs):
    value = lax.ppermute(value, ("row", "col"), pairs)
    return lax.ppermute(value, ("row", "col"), pairs)


def butterfly_sum(value, axis):
    count = lax.axis_size(axis)
    if count & (count - 1):
        return lax.psum(value, axis)
    index = lax.axis_index(axis)
    stride = 1
    while stride < count:
        radix = 4 if count // stride >= 4 else 2
        digit = (index // stride) % radix
        received = [value]
        for shift in range(1, radix):
            pairs = []
            for source in range(count):
                source_digit = (source // stride) % radix
                target = source + (((source_digit + shift) % radix) - source_digit) * stride
                pairs.append((source, target))
            received.append(lax.ppermute(value, axis, pairs))
        received = jnp.stack(received)
        total = received[(digit - 0) % radix]
        for place in range(1, radix):
            total = total + received[(digit - place) % radix]
        value = total
        stride *= radix
    return value


def update(user_fac, user_acc, item_fac, item_acc, rating_block, live_tiles):
    tile_size = user_fac.shape[0] // live_tiles.shape[0]
    user_half = user_fac.astype(jnp.bfloat16)
    item_half = item_fac.astype(jnp.bfloat16)
    predicted = lax.dot_general(
        user_half, item_half, (((1,), (1,)), ((), ())), preferred_element_type=jnp.float32
    )
    residue = predicted - rating_block.astype(jnp.float32)
    masked = (
        residue.reshape(live_tiles.shape[0], tile_size, live_tiles.shape[1], tile_size)
        * live_tiles[:, None, :, None]
    ).reshape(residue.shape)
    sq_error = jnp.sum(masked * residue)
    err_half = masked.astype(jnp.bfloat16)
    grad_user = (
        jnp.dot(err_half, item_half, preferred_element_type=jnp.float32)
        * float(item_fac.shape[0]) ** (-0.5)
        + ridge_weight * user_fac
    )
    grad_item = (
        lax.dot_general(
            err_half, user_half, (((0,), (0,)), ((), ())), preferred_element_type=jnp.float32
        )
        * float(UT * TILE) ** (-0.5)
        + ridge_weight * item_fac
    )
    user_acc = user_acc + grad_user * grad_user
    item_acc = item_acc + grad_item * grad_item
    user_fac = user_fac - step_rate * grad_user * lax.rsqrt(user_acc)
    item_fac = item_fac - step_rate * grad_item * lax.rsqrt(item_acc)
    return (user_fac, user_acc, item_fac, item_acc, sq_error)


def on_device(ratings, tile_mask, tile_counts, users, user_accum, items, item_accum, pairs=None):
    strata_count = ratings.shape[0]
    slot_count = tile_mask.shape[1]
    tile_size = ratings.shape[1] // slot_count
    group_size = lax.axis_size("col")
    member = lax.axis_index("col")
    arrived_rows = users.shape[0]
    group_counts = lax.dynamic_slice_in_dim(
        tile_counts, lax.axis_index("row") * group_size, group_size
    )
    ranks = jnp.arange(group_size, dtype=jnp.int32)
    start_tile = jnp.sum(jnp.where(ranks < member, group_counts, 0))
    own_count = jnp.sum(jnp.where(ranks == member, group_counts, 0))
    valid = (jnp.arange(slot_count, dtype=jnp.int32) < own_count).astype(jnp.float32)
    tiles_each = arrived_rows // tile_size
    group_tiles = group_size * tiles_each
    rank = users.shape[1]
    group_tile = (start_tile + jnp.arange(slot_count, dtype=jnp.int32)) % group_tiles
    whole_fac = lax.all_gather(users, "col", axis=0, tiled=True)
    user_fac = whole_fac.reshape(group_tiles, tile_size, rank)[group_tile].reshape(-1, rank)
    if pairs is None:
        whole_acc = lax.all_gather(user_accum, "col", axis=0, tiled=True)
        user_acc = whole_acc.reshape(group_tiles, tile_size, rank)[group_tile].reshape(-1, rank)
    else:
        partner = core_swap(user_accum)
        far = far_chip(user_accum, pairs)
        far_partner = core_swap(far)
        by_offset = jnp.stack([user_accum, partner, far, far_partner]).reshape(
            group_size, tiles_each, tile_size, rank
        )
        offset = (group_tile // tiles_each) ^ member
        user_acc = by_offset[offset, group_tile % tiles_each].reshape(-1, rank)
    item_fac = items
    item_acc = item_accum
    loss_list = []
    for stratum in range(strata_count):
        live_tiles = tile_mask[stratum].astype(jnp.float32) * valid[:, None]
        for inner in range(STEPS):
            user_fac, user_acc, item_fac, item_acc, sq_error = update(
                user_fac, user_acc, item_fac, item_acc, ratings[stratum], live_tiles
            )
            if inner == 0:
                observed = jnp.sum(live_tiles) * float(tile_size * tile_size)
                loss_list.append(jnp.stack([sq_error, observed]))
        if stratum + 1 < strata_count:
            item_fac, item_acc = passed_along((item_fac, item_acc), ("row", "col"), 1)
    loss_parts = butterfly_sum(jnp.stack(loss_list), ("row", "col"))
    losses = loss_parts[:, 0] / loss_parts[:, 1]
    pad_rows = slot_count * tile_size
    row_valid = jnp.repeat(valid, tile_size)[None, :, None] > 0.5
    kept_pair = jnp.where(row_valid, jnp.stack([user_fac, user_acc]), 0.0)
    frame_rows = group_size * arrived_rows + pad_rows
    frame_pair = lax.dynamic_update_slice_in_dim(
        jnp.zeros((2, frame_rows, rank), jnp.float32), kept_pair, start_tile * tile_size, 1
    )
    if pairs is None:
        users_pair = lax.psum_scatter(
            frame_pair[:, : group_size * arrived_rows], "col", scatter_dimension=1, tiled=True
        )
        users_new, accum_new = users_pair[0], users_pair[1]
    else:
        half_rows = arrived_rows // 2
        fac_blocks = frame_pair[0, : group_size * arrived_rows].reshape(group_size, arrived_rows, rank)
        acc_blocks = frame_pair[1, : group_size * arrived_rows].reshape(group_size, arrived_rows, rank)
        on_sparse = jnp.concatenate([fac_blocks, acc_blocks[:, :half_rows]], axis=1)
        scattered = lax.psum_scatter(
            on_sparse.reshape(-1, rank), "col", scatter_dimension=0, tiled=True
        )
        order = jnp.arange(group_size, dtype=jnp.int32) ^ member
        by_offset = jnp.take(acc_blocks[:, half_rows:], order, axis=0)
        from_partner = core_swap(jnp.stack([by_offset[1], by_offset[3]]))
        cross = by_offset[2] + from_partner[1]
        from_far = far_chip(cross, pairs)
        accum_high = by_offset[0] + from_partner[0] + from_far
        users_new = scattered[:arrived_rows]
        accum_new = jnp.concatenate([scattered[arrived_rows:], accum_high], axis=0)
    return (users_new, accum_new, item_fac, item_acc, losses)


def solution(mesh):
    pairs = None
    if mesh.devices.shape[1] == 4 and hasattr(mesh.devices.flat[0], "coords"):
        pairs = z_shift_pairs(mesh)
    return jax.shard_map(
        partial(on_device, pairs=pairs),
        mesh=mesh,
        in_specs=(
            P(None, ("row", "col"), None),
            P(None, ("row", "col"), None),
            P(),
            P(("row", "col"), None),
            P(("row", "col"), None),
            P(("row", "col"), None),
            P(("row", "col"), None),
        ),
        out_specs=(
            P(("row", "col"), None),
            P(("row", "col"), None),
            P(("row", "col"), None),
            P(("row", "col"), None),
            P(),
        ),
        check_vma=False,
    )
```

```python
from functools import partial

import jax
import jax.numpy as jnp
from jax import lax
from jax.sharding import PartitionSpec as P

TILE = 128
UT = 8
STEPS = 3


ridge_weight = 0.02
step_rate = 0.05


def passed_along(value, axis, steps):
    count = lax.axis_size(axis)
    pairs = [(source, (source + steps) % count) for source in range(count)]
    return lax.ppermute(value, axis, pairs)


def z_shift_pairs(mesh):
    grid = mesh.devices
    place = {}
    for row in range(grid.shape[0]):
        for col in range(grid.shape[1]):
            device = grid[row, col]
            place[(*device.coords, device.core_on_chip)] = row * grid.shape[1] + col
    depth = 1 + max(key[2] for key in place)
    pairs = []
    for (x, y, z, core), index in sorted(place.items(), key=lambda item: item[1]):
        step = 1 if core == 0 else -1
        pairs.append((index, place[(x, y, (z + step) % depth, core)]))
    return pairs


def core_swap(value):
    count = lax.axis_size("col")
    return lax.ppermute(value, "col", [(source, source ^ 1) for source in range(count)])


def far_chip(value, pairs):
    value = lax.ppermute(value, ("row", "col"), pairs)
    return lax.ppermute(value, ("row", "col"), pairs)


def butterfly_sum(value, axis):
    count = lax.axis_size(axis)
    if count & (count - 1):
        return lax.psum(value, axis)
    stride = 1
    while stride < count:
        pairs = [(source, source ^ stride) for source in range(count)]
        value = value + lax.ppermute(value, axis, pairs)
        stride *= 2
    return value


def update(user_fac, user_acc, item_fac, item_acc, rating_block, live_tiles):
    tile_size = user_fac.shape[0] // live_tiles.shape[0]
    user_half = user_fac.astype(jnp.bfloat16)
    item_half = item_fac.astype(jnp.bfloat16)
    predicted = lax.dot_general(
        user_half, item_half, (((1,), (1,)), ((), ())), preferred_element_type=jnp.float32
    )
    residue = predicted - rating_block.astype(jnp.float32)
    masked = (
        residue.reshape(live_tiles.shape[0], tile_size, live_tiles.shape[1], tile_size)
        * live_tiles[:, None, :, None]
    ).reshape(residue.shape)
    sq_error = jnp.sum(masked * residue)
    err_half = masked.astype(jnp.bfloat16)
    grad_user = (
        jnp.dot(err_half, item_half, preferred_element_type=jnp.float32)
        * float(item_fac.shape[0]) ** (-0.5)
        + ridge_weight * user_fac
    )
    grad_item = (
        lax.dot_general(
            err_half, user_half, (((0,), (0,)), ((), ())), preferred_element_type=jnp.float32
        )
        * float(UT * TILE) ** (-0.5)
        + ridge_weight * item_fac
    )
    user_acc = user_acc + grad_user * grad_user
    item_acc = item_acc + grad_item * grad_item
    user_fac = user_fac - step_rate * grad_user * lax.rsqrt(user_acc)
    item_fac = item_fac - step_rate * grad_item * lax.rsqrt(item_acc)
    return (user_fac, user_acc, item_fac, item_acc, sq_error)


def on_device(ratings, tile_mask, tile_counts, users, user_accum, items, item_accum, pairs=None):
    strata_count = ratings.shape[0]
    slot_count = tile_mask.shape[1]
    tile_size = ratings.shape[1] // slot_count
    group_size = lax.axis_size("col")
    member = lax.axis_index("col")
    arrived_rows = users.shape[0]
    group_counts = lax.dynamic_slice_in_dim(
        tile_counts, lax.axis_index("row") * group_size, group_size
    )
    ranks = jnp.arange(group_size, dtype=jnp.int32)
    start_tile = jnp.sum(jnp.where(ranks < member, group_counts, 0))
    own_count = jnp.sum(jnp.where(ranks == member, group_counts, 0))
    valid = (jnp.arange(slot_count, dtype=jnp.int32) < own_count).astype(jnp.float32)
    tiles_each = arrived_rows // tile_size
    group_tiles = group_size * tiles_each
    rank = users.shape[1]
    group_tile = (start_tile + jnp.arange(slot_count, dtype=jnp.int32)) % group_tiles
    whole_fac = lax.all_gather(users, "col", axis=0, tiled=True)
    user_fac = whole_fac.reshape(group_tiles, tile_size, rank)[group_tile].reshape(-1, rank)
    if pairs is None:
        whole_acc = lax.all_gather(user_accum, "col", axis=0, tiled=True)
        user_acc = whole_acc.reshape(group_tiles, tile_size, rank)[group_tile].reshape(-1, rank)
    else:
        partner = core_swap(user_accum)
        far = far_chip(user_accum, pairs)
        far_partner = core_swap(far)
        by_offset = jnp.stack([user_accum, partner, far, far_partner]).reshape(
            group_size, tiles_each, tile_size, rank
        )
        offset = (group_tile // tiles_each) ^ member
        user_acc = by_offset[offset, group_tile % tiles_each].reshape(-1, rank)
    item_fac = items
    item_acc = item_accum
    loss_list = []
    for stratum in range(strata_count):
        live_tiles = tile_mask[stratum].astype(jnp.float32) * valid[:, None]
        for inner in range(STEPS):
            user_fac, user_acc, item_fac, item_acc, sq_error = update(
                user_fac, user_acc, item_fac, item_acc, ratings[stratum], live_tiles
            )
            if inner == 0:
                observed = jnp.sum(live_tiles) * float(tile_size * tile_size)
                loss_list.append(jnp.stack([sq_error, observed]))
        if stratum + 1 < strata_count:
            item_fac = passed_along(item_fac, ("row", "col"), 1)
            item_fac, item_acc = lax.optimization_barrier((item_fac, item_acc))
            item_acc = passed_along(item_acc, ("row", "col"), 1)
    loss_parts = butterfly_sum(jnp.stack(loss_list), ("row", "col"))
    losses = loss_parts[:, 0] / loss_parts[:, 1]
    pad_rows = slot_count * tile_size
    row_valid = jnp.repeat(valid, tile_size)[None, :, None] > 0.5
    kept_pair = jnp.where(row_valid, jnp.stack([user_fac, user_acc]), 0.0)
    frame_rows = group_size * arrived_rows + pad_rows
    frame_pair = lax.dynamic_update_slice_in_dim(
        jnp.zeros((2, frame_rows, rank), jnp.float32), kept_pair, start_tile * tile_size, 1
    )
    users_pair = lax.psum_scatter(
        frame_pair[:, : group_size * arrived_rows], "col", scatter_dimension=1, tiled=True
    )
    return (users_pair[0], users_pair[1], item_fac, item_acc, losses)


def solution(mesh):
    pairs = None
    if mesh.devices.shape[1] == 4 and hasattr(mesh.devices.flat[0], "coords"):
        pairs = z_shift_pairs(mesh)
    return jax.shard_map(
        partial(on_device, pairs=pairs),
        mesh=mesh,
        in_specs=(
            P(None, ("row", "col"), None),
            P(None, ("row", "col"), None),
            P(),
            P(("row", "col"), None),
            P(("row", "col"), None),
            P(("row", "col"), None),
            P(("row", "col"), None),
        ),
        out_specs=(
            P(("row", "col"), None),
            P(("row", "col"), None),
            P(("row", "col"), None),
            P(("row", "col"), None),
            P(),
        ),
        check_vma=False,
    )
```

```python
from functools import partial

import jax
import jax.numpy as jnp
from jax import lax
from jax.sharding import PartitionSpec as P

TILE = 128
UT = 8
STEPS = 3


ridge_weight = 0.02
step_rate = 0.05


def passed_along(value, axis, steps):
    count = lax.axis_size(axis)
    pairs = [(source, (source + steps) % count) for source in range(count)]
    return lax.ppermute(value, axis, pairs)


def z_shift_pairs(mesh):
    grid = mesh.devices
    place = {}
    for row in range(grid.shape[0]):
        for col in range(grid.shape[1]):
            device = grid[row, col]
            place[(*device.coords, device.core_on_chip)] = row * grid.shape[1] + col
    depth = 1 + max(key[2] for key in place)
    pairs = []
    for (x, y, z, core), index in sorted(place.items(), key=lambda item: item[1]):
        step = 1 if core == 0 else -1
        pairs.append((index, place[(x, y, (z + step) % depth, core)]))
    return pairs


def core_swap(value):
    count = lax.axis_size("col")
    return lax.ppermute(value, "col", [(source, source ^ 1) for source in range(count)])


def far_chip(value, pairs):
    value = lax.ppermute(value, ("row", "col"), pairs)
    return lax.ppermute(value, ("row", "col"), pairs)


def butterfly_sum(value, axis):
    count = lax.axis_size(axis)
    if count & (count - 1):
        return lax.psum(value, axis)
    stride = 1
    while stride < count:
        pairs = [(source, source ^ stride) for source in range(count)]
        value = value + lax.ppermute(value, axis, pairs)
        stride *= 2
    return value


def update(user_fac, user_acc, item_fac, item_acc, rating_block, live_tiles):
    tile_size = user_fac.shape[0] // live_tiles.shape[0]
    user_half = user_fac.astype(jnp.bfloat16)
    item_half = item_fac.astype(jnp.bfloat16)
    predicted = lax.dot_general(
        user_half, item_half, (((1,), (1,)), ((), ())), preferred_element_type=jnp.float32
    )
    residue = predicted - rating_block.astype(jnp.float32)
    masked = (
        residue.reshape(live_tiles.shape[0], tile_size, live_tiles.shape[1], tile_size)
        * live_tiles[:, None, :, None]
    ).reshape(residue.shape)
    sq_error = jnp.sum(masked * residue)
    err_half = masked.astype(jnp.bfloat16)
    grad_user = (
        jnp.dot(err_half, item_half, preferred_element_type=jnp.float32)
        * float(item_fac.shape[0]) ** (-0.5)
        + ridge_weight * user_fac
    )
    grad_item = (
        lax.dot_general(
            err_half, user_half, (((0,), (0,)), ((), ())), preferred_element_type=jnp.float32
        )
        * float(UT * TILE) ** (-0.5)
        + ridge_weight * item_fac
    )
    user_acc = user_acc + grad_user * grad_user
    item_acc = item_acc + grad_item * grad_item
    user_fac = user_fac - step_rate * grad_user * lax.rsqrt(user_acc)
    item_fac = item_fac - step_rate * grad_item * lax.rsqrt(item_acc)
    return (user_fac, user_acc, item_fac, item_acc, sq_error)


def on_device(ratings, tile_mask, tile_counts, users, user_accum, items, item_accum, pairs=None):
    strata_count = ratings.shape[0]
    slot_count = tile_mask.shape[1]
    tile_size = ratings.shape[1] // slot_count
    group_size = lax.axis_size("col")
    member = lax.axis_index("col")
    arrived_rows = users.shape[0]
    group_counts = lax.dynamic_slice_in_dim(
        tile_counts, lax.axis_index("row") * group_size, group_size
    )
    ranks = jnp.arange(group_size, dtype=jnp.int32)
    start_tile = jnp.sum(jnp.where(ranks < member, group_counts, 0))
    own_count = jnp.sum(jnp.where(ranks == member, group_counts, 0))
    valid = (jnp.arange(slot_count, dtype=jnp.int32) < own_count).astype(jnp.float32)
    tiles_each = arrived_rows // tile_size
    group_tiles = group_size * tiles_each
    rank = users.shape[1]
    group_tile = (start_tile + jnp.arange(slot_count, dtype=jnp.int32)) % group_tiles
    whole_acc = lax.all_gather(user_accum, "col", axis=0, tiled=True)
    user_acc = whole_acc.reshape(group_tiles, tile_size, rank)[group_tile].reshape(-1, rank)
    if pairs is None:
        whole_fac = lax.all_gather(users, "col", axis=0, tiled=True)
        user_fac = whole_fac.reshape(group_tiles, tile_size, rank)[group_tile].reshape(-1, rank)
    else:
        partner = core_swap(users)
        far = far_chip(users, pairs)
        far_partner = core_swap(far)
        by_offset = jnp.stack([users, partner, far, far_partner]).reshape(
            group_size, tiles_each, tile_size, rank
        )
        offset = (group_tile // tiles_each) ^ member
        user_fac = by_offset[offset, group_tile % tiles_each].reshape(-1, rank)
    item_fac = items
    item_acc = item_accum
    loss_list = []
    for stratum in range(strata_count):
        live_tiles = tile_mask[stratum].astype(jnp.float32) * valid[:, None]
        for inner in range(STEPS):
            user_fac, user_acc, item_fac, item_acc, sq_error = update(
                user_fac, user_acc, item_fac, item_acc, ratings[stratum], live_tiles
            )
            if inner == 0:
                observed = jnp.sum(live_tiles) * float(tile_size * tile_size)
                loss_list.append(jnp.stack([sq_error, observed]))
        if stratum + 1 < strata_count:
            item_fac, item_acc = passed_along((item_fac, item_acc), ("row", "col"), 1)
    loss_parts = butterfly_sum(jnp.stack(loss_list), ("row", "col"))
    losses = loss_parts[:, 0] / loss_parts[:, 1]
    pad_rows = slot_count * tile_size
    row_valid = jnp.repeat(valid, tile_size)[None, :, None] > 0.5
    kept_pair = jnp.where(row_valid, jnp.stack([user_fac, user_acc]), 0.0)
    frame_rows = group_size * arrived_rows + pad_rows
    frame_pair = lax.dynamic_update_slice_in_dim(
        jnp.zeros((2, frame_rows, rank), jnp.float32), kept_pair, start_tile * tile_size, 1
    )
    users_pair = lax.psum_scatter(
        frame_pair[:, : group_size * arrived_rows], "col", scatter_dimension=1, tiled=True
    )
    return (users_pair[0], users_pair[1], item_fac, item_acc, losses)


def solution(mesh):
    pairs = None
    if mesh.devices.shape[1] == 4 and hasattr(mesh.devices.flat[0], "coords"):
        pairs = z_shift_pairs(mesh)
    return jax.shard_map(
        partial(on_device, pairs=pairs),
        mesh=mesh,
        in_specs=(
            P(None, ("row", "col"), None),
            P(None, ("row", "col"), None),
            P(),
            P(("row", "col"), None),
            P(("row", "col"), None),
            P(("row", "col"), None),
            P(("row", "col"), None),
        ),
        out_specs=(
            P(("row", "col"), None),
            P(("row", "col"), None),
            P(("row", "col"), None),
            P(("row", "col"), None),
            P(),
        ),
        check_vma=False,
    )
```
